512 devices in a mesh: dp: 32 (over y, x), ctx: 16 (over z, core).
Axes of the slice: x: 4, y: 8, z: 8, core: 2. Of those that a mesh axis runs over, the one named last changes fastest.
Arguments:
- xbc: bfloat16 [65536, 3328], P(('dp', 'ctx')), parts along dimension 0, may hold values from -6 to 6
- dt_raw: float32 [65536, 48], P(('dp', 'ctx')), parts along dimension 0, may hold values from -3 to 3
- lengths: int32 [256], P('dp'), parts along dimension 0, may hold values from 1 to 1024, 2048 in all
- conv_weight: float32 [4, 3328], replicated, may hold values from -3 to 3
- conv_bias: float32 [3328], replicated, may hold values from -3 to 3
- dt_bias: float32 [48], replicated, may hold values from -1 to 1
- decay_rate: float32 [48], replicated, may hold values from 0.0001 to 0.08
- skip: float32 [48], replicated, may hold values from 0.5 to 4
- norm_gain: float32 [3072], replicated, may hold values from 0.5 to 1.5
Outputs:
- mixed: bfloat16 [65536, 3072], P(('dp', 'ctx')), parts along dimension 0
The draws below stay inside these ranges and needn't reach their ends.
There are 32 independent parts, one for each index of `dp`. The reference program is written for one: setup_inputs(seed, part) draws one part's arguments, and reference() takes and returns one part's arrays. A program takes and returns all parts, laid end to end along the dimension named above; an argument that names none is the same for every part. Nothing has to cross between parts.
Inputs may be any that keep to these rules, and one draw needn't show every extreme that they name: Documents lie end to end in order and their lengths sum to 2048; the longest is exactly 1024.
All inputs are finite; a program needn't handle non-finite values.
Results may differ from the reference program's by a relative error of at most 0.0036.
Values may be sent and summed in bfloat16 or wider, within the bound.
No kernel may reach another device: no remote copies, remote signals or barrier semaphores. Data moves between devices by JAX's collectives and lax.ppermute only.
A program may use at most 128 MiB of HBM per device.

```python
import math
import jax
import jax.numpy as jnp
import numpy as np
from jax import lax

HEADS = 48
HEAD_DIM = 64
STATE = 128
CONV = 4
DOCS = 8
TOK_DEV = 128
SEQ = 2048
INNER = 3072
CH = 3328


def draw_decay_rate(key, part):
    first, second, third = jax.random.split(key, 3)
    slow = jnp.exp(jnp.log(0.0001) + jax.random.uniform(first, (HEADS,), jnp.float32) * jnp.log(4.0))
    quick = jnp.exp(jnp.log(0.0004) + jax.random.uniform(second, (HEADS,), jnp.float32) * jnp.log(200.0))
    picked = jax.random.uniform(third, (HEADS,), jnp.float32) < 0.5
    return jnp.where(picked, slow, quick).astype(jnp.float32)


def steps_of(own_key, dims, cuts, least, top_value):
    loudness, own = 1.0, jax.random.fold_in(own_key, 6)
    for axis_at, shards_of in cuts:
        heights = jnp.exp(jax.random.uniform(jax.random.fold_in(own, axis_at), (shards_of,), jnp.float32, least / len(cuts), top_value / len(cuts)))
        loudness = loudness * jnp.repeat(heights, dims[axis_at] // shards_of).reshape([-1 if axis == axis_at else 1 for axis in range(len(dims))])
    return loudness


def split_up(amount, total, bound, slope):
    loads = [(1 << 20) // math.isqrt(rank ** slope) + 1 for rank in range(2, amount + 1)]
    rest, counts = total - bound - (amount - 1), [1] * (amount - 1)
    while rest > 0:
        movable = [i for i in range(amount - 1) if counts[i] < bound]
        pool, remaining = sum([loads[i] for i in movable]), rest
        for i in movable:
            more = min(bound - counts[i], max(1, remaining * loads[i] // pool), rest)
            counts[i] = counts[i] + more
            rest = rest - more
    return np.array([bound] + counts)


def ragged_sizes(own_key, number_of, total, bound, skew):
    if number_of == 2:
        one = jax.random.randint(own_key, (), max(1, total - bound), min(bound, total - 1) + 1)
        return jnp.stack([one, total - one])
    tallies = jnp.asarray(split_up(number_of, total, bound, skew), jnp.int32)
    pairs = (number_of - 1) // 2
    giver, taker = tallies[1:1 + 2 * pairs:2], tallies[2:2 + 2 * pairs:2]
    room = jnp.minimum(giver - 1, bound - taker)
    moved = jax.random.randint(jax.random.fold_in(own_key, 1), (pairs,), 0, 1 << 20) % (room + 1)
    tallies = tallies.at[1:1 + 2 * pairs:2].set(giver - moved).at[2:2 + 2 * pairs:2].set(taker + moved)
    return tallies[jax.random.permutation(jax.random.fold_in(own_key, 2), number_of)]


def noise(stream_key, dims, scale, most, cuts=(), kind=jnp.bfloat16):
    array = jax.random.normal(stream_key, dims, jnp.float32) * scale
    if len(cuts) > 0:
        array = steps_of(stream_key, dims, cuts, -0.22, 0.18) * array
    return jnp.clip(array, min=-most, max=most).astype(kind)


def setup_inputs(seed: int = 0, part: int = 0) -> dict:
    streams_of = jax.random.split(jax.random.key(seed), 10)
    part_keys = jax.random.split(jax.random.fold_in(streams_of[9], part), 10)
    xbc = noise(part_keys[0], (SEQ, CH), 1.0, 6.0, ((0, 16),))
    dt_raw = noise(part_keys[1], (SEQ, HEADS), 0.5, 3.0, ((0, 16),), jnp.float32)
    lengths = ragged_sizes(part_keys[2], DOCS, SEQ, SEQ // 2, 2).astype(jnp.int32)
    conv_weight = noise(streams_of[3], (CONV, CH), 0.5, 3.0, (), jnp.float32)
    conv_bias = noise(streams_of[4], (CH,), 0.5, 3.0, (), jnp.float32)
    dt_bias = jnp.clip(jax.random.uniform(streams_of[5], (HEADS,), jnp.float32, -1.0, 1.0), -1.0, 1.0)
    decay_rate = draw_decay_rate(jax.random.fold_in(streams_of[9], 71), part)
    skip = jnp.clip(jnp.exp(jax.random.uniform(streams_of[7], (HEADS,), jnp.float32, math.log(0.5), math.log(4.0))), 0.5, 4.0)
    norm_gain = jnp.clip(1.0 + 0.1 * jax.random.normal(streams_of[8], (INNER,), jnp.float32), 0.5, 1.5)
    return dict(xbc=xbc, dt_raw=dt_raw, lengths=lengths, conv_weight=conv_weight, conv_bias=conv_bias, dt_bias=dt_bias, decay_rate=decay_rate, skip=skip, norm_gain=norm_gain)


def positions_info(lengths):
    ends = jnp.cumsum(lengths).astype(jnp.int32)
    places = jnp.arange(SEQ, dtype=jnp.int32)
    seg = lax.optimization_barrier(jnp.sum((places[:, None] >= ends[None, :]).astype(jnp.int32), axis=1)).astype(jnp.int32)
    before = jnp.concatenate([jnp.full((1,), -1, jnp.int32), seg[:-1]])
    return (seg, seg != before)

def reference(xbc, dt_raw, lengths, conv_weight, conv_bias, dt_bias, decay_rate, skip, norm_gain):
    seg, start = positions_info(lengths)
    raw = xbc.astype(jnp.float32)
    total = conv_bias[None, :] + conv_weight[CONV - 1][None, :] * raw
    for lag in range(1, CONV):
        moved = jnp.concatenate([jnp.zeros((lag, raw.shape[1]), jnp.float32), raw[:-lag]])
        earlier = jnp.concatenate([jnp.full((lag,), -1, jnp.int32), seg[:-lag]])
        total = total + conv_weight[CONV - 1 - lag][None, :] * jnp.where((earlier == seg)[:, None], moved, 0.0)
    act = jax.nn.silu(total).astype(jnp.bfloat16)
    step_size = jax.nn.softplus(dt_raw + dt_bias[None, :])
    log_decay = -step_size * decay_rate[None, :]
    blocks = SEQ // TOK_DEV

    def split(arr):
        return arr.reshape((blocks, TOK_DEV) + arr.shape[1:])
    index = jnp.arange(TOK_DEV, dtype=jnp.int32)
    gains = norm_gain.reshape(HEADS, HEAD_DIM)

    def advance(carry, items):
        block_act, block_dt, block_log, block_seg, block_start = items
        xs = block_act[:, :INNER].reshape(TOK_DEV, HEADS, HEAD_DIM)
        bs = block_act[:, INNER:INNER + STATE]
        cs = block_act[:, INNER + STATE:]
        cum = jnp.cumsum(block_log, axis=0)
        alive = (jnp.cumsum(block_start.astype(jnp.int32)) == 0).astype(jnp.float32)
        scores = jnp.dot(cs, bs.T, preferred_element_type=jnp.float32)
        mask = (index[:, None] >= index[None, :]) & (block_seg[:, None] == block_seg[None, :])
        diff = cum[:, None, :] - cum[None, :, :]
        decay = jnp.where(mask[:, :, None], jnp.exp(jnp.where(mask[:, :, None], diff, 0.0)), 0.0)
        weights = (scores[:, :, None] * decay * block_dt[None, :, :]).astype(jnp.bfloat16)
        inner = jnp.einsum('tsh,shp->thp', weights.astype(jnp.float32), xs.astype(jnp.float32))
        carried = lax.optimization_barrier(carry.astype(jnp.bfloat16)).astype(jnp.float32)
        outer = jnp.exp(cum)[:, :, None] * alive[:, None, None] * jnp.einsum('hpn,tn->thp', carried, cs.astype(jnp.float32))
        same_end = (block_seg == block_seg[-1]).astype(jnp.float32)
        factor = jnp.exp(cum[-1][None, :] - cum) * same_end[:, None] * block_dt
        scaled = (factor[:, :, None] * xs.astype(jnp.float32)).astype(jnp.bfloat16)
        local = jnp.einsum('shp,sn->hpn', scaled.astype(jnp.float32), bs.astype(jnp.float32))
        block_decay = jnp.exp(cum[-1]) * alive[-1]
        renewed = block_decay[:, None, None] * carry + local
        total_out = inner + outer + skip[None, :, None] * xs.astype(jnp.float32)
        normed = total_out * lax.rsqrt(lax.optimization_barrier(jnp.mean(total_out * total_out, axis=-1, keepdims=True)) + 1e-05) * gains[None]
        return (renewed, normed.astype(jnp.bfloat16).reshape(TOK_DEV, INNER))
    start_state = jnp.zeros((HEADS, HEAD_DIM, STATE), jnp.float32)
    items = (split(act), split(step_size), split(log_decay), split(seg), split(start))
    final, outputs = lax.scan(advance, start_state, items)
    return outputs.reshape(SEQ, INNER)
```

```python
import jax
import jax.numpy as jnp
from jax import lax
from jax.sharding import PartitionSpec as P


def shifted(block, axis, distance):
    devices = range(lax.axis_size(axis))
    route = [(i - distance, i) for i in devices if i - distance in devices]
    return lax.ppermute(block, axis, route)


def chain_carry(decay, local, chunks):
    size, position = (lax.axis_size("ctx"), lax.axis_index("ctx"))
    chips = size // 2
    chip = position // 2
    heads = decay.shape[0]
    width = heads // chunks
    up = [(2 * i, 2 * i + 1) for i in range(chips)]
    down = [(2 * i + 1, 2 * i) for i in range(chips)]
    ahead = [(2 * i + 1, 2 * i + 3) for i in range(chips - 1)]
    decay_low, local_low = lax.ppermute((decay, local), "ctx", up)
    chip_decay = decay * decay_low
    chip_local = decay[:, None, None] * local_low + local
    received = jnp.zeros((width,) + local.shape[1:], local.dtype)
    carry = jnp.zeros_like(local)
    for step in range(chunks + chips - 1):
        k = step - chip
        valid = (k >= 0) & (k < chunks)
        at = jnp.clip(k, 0, chunks - 1) * width
        old = lax.dynamic_slice_in_dim(carry, at, width, 0)
        carry = lax.dynamic_update_slice_in_dim(carry, jnp.where(valid, received, old), at, 0)
        if step < chunks + chips - 2:
            d = lax.dynamic_slice_in_dim(chip_decay, at, width, 0)
            l = lax.dynamic_slice_in_dim(chip_local, at, width, 0)
            received = lax.ppermute(d[:, None, None] * received + l, "ctx", ahead)
    lowered = lax.ppermute(carry, "ctx", down)
    own = decay_low[:, None, None] * carry + local_low
    return jnp.where(position % 2 == 0, lowered, own)


def body(xbc, dt_raw, lengths, conv_weight, conv_bias, dt_bias, decay_rate, skip, norm_gain):
    rows = xbc.shape[0]
    heads = dt_raw.shape[1]
    inner_width = norm_gain.shape[0]
    head_dim = inner_width // heads
    state_dim = (xbc.shape[1] - inner_width) // 2
    taps = conv_weight.shape[0]
    device = lax.axis_index("ctx")
    first = device * rows
    ends = jnp.cumsum(lengths)
    places = first - (taps - 1) + jnp.arange(rows + taps - 1, dtype=jnp.int32)
    counted = jnp.sum((places[:, None] >= ends[None, :]).astype(jnp.int32), axis=1)
    seg_wide = jnp.where(places < 0, -1, counted)
    seg = seg_wide[taps - 1 :]
    start = seg != seg_wide[taps - 2 : -1]
    rim = shifted(xbc[rows - (taps - 1) :], "ctx", 1)
    widened = jnp.concatenate([rim, xbc], axis=0)
    total = conv_bias[None, :] + conv_weight[taps - 1][None, :] * xbc.astype(jnp.float32)
    for lag in range(1, taps):
        moved = widened[taps - 1 - lag : taps - 1 - lag + rows].astype(jnp.float32)
        same = seg_wide[taps - 1 - lag : taps - 1 - lag + rows] == seg
        total = total + conv_weight[taps - 1 - lag][None, :] * jnp.where(same[:, None], moved, 0.0)
    act = jax.nn.silu(total).astype(jnp.bfloat16)
    xs = act[:, :inner_width].reshape(rows, heads, head_dim)
    bs = act[:, inner_width : inner_width + state_dim]
    cs = act[:, inner_width + state_dim :]
    step_size = jax.nn.softplus(dt_raw + dt_bias[None, :])
    cum = jnp.cumsum(-step_size * decay_rate[None, :], axis=0)
    alive = (jnp.cumsum(start.astype(jnp.int32)) == 0).astype(jnp.float32)
    same_end = (seg == seg[-1]).astype(jnp.float32)
    factor = jnp.exp(cum[-1][None, :] - cum) * same_end[:, None] * step_size
    scaled = (factor[:, :, None] * xs.astype(jnp.float32)).astype(jnp.bfloat16)
    local = jnp.einsum("shp,sn->hpn", scaled, bs, preferred_element_type=jnp.float32)
    block_decay = jnp.exp(cum[-1]) * alive[-1]
    scores = jnp.dot(cs, bs.T, preferred_element_type=jnp.float32)
    index = jnp.arange(rows, dtype=jnp.int32)
    mask = (index[:, None] >= index[None, :]) & (seg[:, None] == seg[None, :])
    group = 8
    pieces = []
    for part_start in range(0, heads, group):
        cum_part = cum[:, part_start : part_start + group].T
        diff = cum_part[:, :, None] - cum_part[:, None, :]
        decay = jnp.where(mask[None], jnp.exp(jnp.where(mask[None], diff, 0.0)), 0.0)
        weights = (
            scores[None] * decay * step_size[:, part_start : part_start + group].T[:, None, :]
        ).astype(jnp.bfloat16)
        pieces.append(
            jnp.einsum(
                "hts,shp->thp",
                weights,
                xs[:, part_start : part_start + group, :],
                preferred_element_type=jnp.float32,
            )
        )
    inner = jnp.concatenate(pieces, axis=1)
    carry = chain_carry(block_decay, local, 4)
    carried = carry.astype(jnp.bfloat16)
    outer = (
        jnp.exp(cum)[:, :, None]
        * alive[:, None, None]
        * jnp.einsum("hpn,tn->thp", carried, cs, preferred_element_type=jnp.float32)
    )
    total_out = inner + outer + skip[None, :, None] * xs.astype(jnp.float32)
    normed = (
        total_out
        * lax.rsqrt(jnp.mean(total_out * total_out, axis=-1, keepdims=True) + 1e-05)
        * norm_gain.reshape(heads, head_dim)[None]
    )
    return normed.astype(jnp.bfloat16).reshape(rows, inner_width)


def solution(mesh):
    in_specs = (
        P(("dp", "ctx"), None),
        P(("dp", "ctx"), None),
        P("dp"),
        P(),
        P(),
        P(),
        P(),
        P(),
        P(),
    )
    out_specs = P(("dp", "ctx"), None)
    return jax.shard_map(body, mesh=mesh, in_specs=in_specs, out_specs=out_specs, check_vma=False)
```

```python
import jax
import jax.numpy as jnp
from jax import lax
from jax.sharding import PartitionSpec as P


def shifted(block, axis, distance):
    devices = range(lax.axis_size(axis))
    route = [(i - distance, i) for i in devices if i - distance in devices]
    return lax.ppermute(block, axis, route)


def chain_carry(decay, local, chunks):
    size, position = (lax.axis_size("ctx"), lax.axis_index("ctx"))
    chips = size // 2
    chip = position // 2
    core = position % 2
    low = core == 0
    heads = decay.shape[0]
    half = heads // 2
    width = half // chunks
    rest = local.shape[1:]
    swap = [(2 * i + j, 2 * i + 1 - j) for i in range(chips) for j in range(2)]
    ahead = [(i, i + 2) for i in range(size - 2)]
    mine = lax.dynamic_slice_in_dim(local, core * half, half, 0)
    theirs = lax.dynamic_slice_in_dim(local, (1 - core) * half, half, 0)
    got_local = lax.ppermute(theirs, "ctx", swap)
    got_decay = lax.ppermute(decay, "ctx", swap)
    decay_hi = lax.dynamic_slice_in_dim(jnp.where(low, got_decay, decay), core * half, half, 0)
    decay_lo = lax.dynamic_slice_in_dim(jnp.where(low, decay, got_decay), core * half, half, 0)
    local_lo = jnp.where(low, mine, got_local)
    local_hi = jnp.where(low, got_local, mine)
    chip_decay = jnp.roll((decay_hi * decay_lo).reshape(chunks, width), chip, axis=0)
    chip_local = jnp.roll(
        (decay_hi[:, None, None] * local_lo + local_hi).reshape((chunks, width) + rest), chip, axis=0
    )
    received = jnp.zeros((width,) + rest, local.dtype)
    slots = [received] * chunks
    for step in range(chunks + chips - 1):
        k = step - chip
        valid = (k >= 0) & (k < chunks)
        j = step % chunks
        slots[j] = jnp.where(valid, received, slots[j])
        if step < chunks + chips - 2:
            received = lax.ppermute(
                chip_decay[j][:, None, None] * received + chip_local[j], "ctx", ahead
            )
    carry_half = jnp.roll(jnp.stack(slots), -chip, axis=0).reshape((half,) + rest)
    onward = decay_lo[:, None, None] * carry_half + local_lo
    got_end = lax.ppermute(jnp.where(low, onward, carry_half), "ctx", swap)
    first = jnp.where(low, carry_half, got_end)
    second = jnp.where(low, got_end, onward)
    return jnp.concatenate([first, second], axis=0)


def body(xbc, dt_raw, lengths, conv_weight, conv_bias, dt_bias, decay_rate, skip, norm_gain):
    rows = xbc.shape[0]
    heads = dt_raw.shape[1]
    inner_width = norm_gain.shape[0]
    head_dim = inner_width // heads
    state_dim = (xbc.shape[1] - inner_width) // 2
    taps = conv_weight.shape[0]
    device = lax.axis_index("ctx")
    first = device * rows
    ends = jnp.cumsum(lengths)
    places = first - (taps - 1) + jnp.arange(rows + taps - 1, dtype=jnp.int32)
    counted = jnp.sum((places[:, None] >= ends[None, :]).astype(jnp.int32), axis=1)
    seg_wide = jnp.where(places < 0, -1, counted)
    seg = seg_wide[taps - 1 :]
    start = seg != seg_wide[taps - 2 : -1]
    rim = shifted(xbc[rows - (taps - 1) :], "ctx", 1)
    widened = jnp.concatenate([rim, xbc], axis=0)
    total = conv_bias[None, :] + conv_weight[taps - 1][None, :] * xbc.astype(jnp.float32)
    for lag in range(1, taps):
        moved = widened[taps - 1 - lag : taps - 1 - lag + rows].astype(jnp.float32)
        same = seg_wide[taps - 1 - lag : taps - 1 - lag + rows] == seg
        total = total + conv_weight[taps - 1 - lag][None, :] * jnp.where(same[:, None], moved, 0.0)
    act = jax.nn.silu(total).astype(jnp.bfloat16)
    xs = act[:, :inner_width].reshape(rows, heads, head_dim)
    bs = act[:, inner_width : inner_width + state_dim]
    cs = act[:, inner_width + state_dim :]
    step_size = jax.nn.softplus(dt_raw + dt_bias[None, :])
    cum = jnp.cumsum(-step_size * decay_rate[None, :], axis=0)
    alive = (jnp.cumsum(start.astype(jnp.int32)) == 0).astype(jnp.float32)
    same_end = (seg == seg[-1]).astype(jnp.float32)
    factor = jnp.exp(cum[-1][None, :] - cum) * same_end[:, None] * step_size
    scaled = (factor[:, :, None] * xs.astype(jnp.float32)).astype(jnp.bfloat16)
    local = jnp.einsum("shp,sn->hpn", scaled, bs, preferred_element_type=jnp.float32)
    block_decay = jnp.exp(cum[-1]) * alive[-1]
    scores = jnp.dot(cs, bs.T, preferred_element_type=jnp.float32)
    index = jnp.arange(rows, dtype=jnp.int32)
    mask = (index[:, None] >= index[None, :]) & (seg[:, None] == seg[None, :])
    group = 8
    pieces = []
    for part_start in range(0, heads, group):
        cum_part = cum[:, part_start : part_start + group].T
        diff = cum_part[:, :, None] - cum_part[:, None, :]
        decay = jnp.where(mask[None], jnp.exp(jnp.where(mask[None], diff, 0.0)), 0.0)
        weights = (
            scores[None] * decay * step_size[:, part_start : part_start + group].T[:, None, :]
        ).astype(jnp.bfloat16)
        pieces.append(
            jnp.einsum(
                "hts,shp->thp",
                weights,
                xs[:, part_start : part_start + group, :],
                preferred_element_type=jnp.float32,
            )
        )
    inner = jnp.concatenate(pieces, axis=1)
    carry = chain_carry(block_decay, local, 4)
    carried = carry.astype(jnp.bfloat16)
    outer = (
        jnp.exp(cum)[:, :, None]
        * alive[:, None, None]
        * jnp.einsum("hpn,tn->thp", carried, cs, preferred_element_type=jnp.float32)
    )
    total_out = inner + outer + skip[None, :, None] * xs.astype(jnp.float32)
    normed = (
        total_out
        * lax.rsqrt(jnp.mean(total_out * total_out, axis=-1, keepdims=True) + 1e-05)
        * norm_gain.reshape(heads, head_dim)[None]
    )
    return normed.astype(jnp.bfloat16).reshape(rows, inner_width)


def solution(mesh):
    in_specs = (
        P(("dp", "ctx"), None),
        P(("dp", "ctx"), None),
        P("dp"),
        P(),
        P(),
        P(),
        P(),
        P(),
        P(),
    )
    out_specs = P(("dp", "ctx"), None)
    return jax.shard_map(body, mesh=mesh, in_specs=in_specs, out_specs=out_specs, check_vma=False)
```

```python
import jax
import jax.numpy as jnp
from jax import lax
from jax.sharding import PartitionSpec as P


def shifted(block, axis, distance):
    devices = range(lax.axis_size(axis))
    route = [(i - distance, i) for i in devices if i - distance in devices]
    return lax.ppermute(block, axis, route)


def chain_carry(decay, local):
    size, position = (lax.axis_size("ctx"), lax.axis_index("ctx"))
    chips = size // 2
    chip = position // 2
    core = position % 2
    low = core == 0
    heads = decay.shape[0]
    half = heads // 2
    rest = local.shape[1:]
    swap = [(2 * i + j, 2 * i + 1 - j) for i in range(chips) for j in range(2)]
    mine = lax.dynamic_slice_in_dim(local, core * half, half, 0)
    theirs = lax.dynamic_slice_in_dim(local, (1 - core) * half, half, 0)
    got_local = lax.ppermute(theirs, "ctx", swap)
    got_decay = lax.ppermute(decay, "ctx", swap)
    decay_hi = lax.dynamic_slice_in_dim(jnp.where(low, got_decay, decay), core * half, half, 0)
    decay_lo = lax.dynamic_slice_in_dim(jnp.where(low, decay, got_decay), core * half, half, 0)
    local_lo = jnp.where(low, mine, got_local)
    local_hi = jnp.where(low, got_local, mine)
    chip_decay = decay_hi * decay_lo
    chip_local = decay_hi[:, None, None] * local_lo + local_hi
    one = [(i, i + 2) for i in range(size - 2)]
    two = [(i, i + 4) for i in range(size - 4)]
    decay_a, local_a = lax.ppermute((chip_decay, chip_local), "ctx", one)
    decay_b, local_b = lax.ppermute((decay_a, local_a), "ctx", one)
    decay_ab = decay_a * decay_b
    local_ab = decay_a[:, None, None] * local_b + local_a
    local_c = lax.ppermute(local_ab, "ctx", two)
    carry_half = decay_ab[:, None, None] * local_c + local_ab
    onward = decay_lo[:, None, None] * carry_half + local_lo
    got_end = lax.ppermute(jnp.where(low, onward, carry_half), "ctx", swap)
    first = jnp.where(low, carry_half, got_end)
    second = jnp.where(low, got_end, onward)
    return jnp.concatenate([first, second], axis=0)


def body(xbc, dt_raw, lengths, conv_weight, conv_bias, dt_bias, decay_rate, skip, norm_gain):
    rows = xbc.shape[0]
    heads = dt_raw.shape[1]
    inner_width = norm_gain.shape[0]
    head_dim = inner_width // heads
    state_dim = (xbc.shape[1] - inner_width) // 2
    taps = conv_weight.shape[0]
    device = lax.axis_index("ctx")
    first = device * rows
    ends = jnp.cumsum(lengths)
    places = first - (taps - 1) + jnp.arange(rows + taps - 1, dtype=jnp.int32)
    counted = jnp.sum((places[:, None] >= ends[None, :]).astype(jnp.int32), axis=1)
    seg_wide = jnp.where(places < 0, -1, counted)
    seg = seg_wide[taps - 1 :]
    start = seg != seg_wide[taps - 2 : -1]
    rim = shifted(xbc[rows - (taps - 1) :], "ctx", 1)
    widened = jnp.concatenate([rim, xbc], axis=0)
    total = conv_bias[None, :] + conv_weight[taps - 1][None, :] * xbc.astype(jnp.float32)
    for lag in range(1, taps):
        moved = widened[taps - 1 - lag : taps - 1 - lag + rows].astype(jnp.float32)
        same = seg_wide[taps - 1 - lag : taps - 1 - lag + rows] == seg
        total = total + conv_weight[taps - 1 - lag][None, :] * jnp.where(same[:, None], moved, 0.0)
    act = jax.nn.silu(total).astype(jnp.bfloat16)
    xs = act[:, :inner_width].reshape(rows, heads, head_dim)
    bs = act[:, inner_width : inner_width + state_dim]
    cs = act[:, inner_width + state_dim :]
    step_size = jax.nn.softplus(dt_raw + dt_bias[None, :])
    cum = jnp.cumsum(-step_size * decay_rate[None, :], axis=0)
    alive = (jnp.cumsum(start.astype(jnp.int32)) == 0).astype(jnp.float32)
    same_end = (seg == seg[-1]).astype(jnp.float32)
    factor = jnp.exp(cum[-1][None, :] - cum) * same_end[:, None] * step_size
    scaled = (factor[:, :, None] * xs.astype(jnp.float32)).astype(jnp.bfloat16)
    local = jnp.einsum("shp,sn->hpn", scaled, bs, preferred_element_type=jnp.float32)
    block_decay = jnp.exp(cum[-1]) * alive[-1]
    scores = jnp.dot(cs, bs.T, preferred_element_type=jnp.float32)
    index = jnp.arange(rows, dtype=jnp.int32)
    mask = (index[:, None] >= index[None, :]) & (seg[:, None] == seg[None, :])
    group = 8
    pieces = []
    for part_start in range(0, heads, group):
        cum_part = cum[:, part_start : part_start + group].T
        diff = cum_part[:, :, None] - cum_part[:, None, :]
        decay = jnp.where(mask[None], jnp.exp(jnp.where(mask[None], diff, 0.0)), 0.0)
        weights = (
            scores[None] * decay * step_size[:, part_start : part_start + group].T[:, None, :]
        ).astype(jnp.bfloat16)
        pieces.append(
            jnp.einsum(
                "hts,shp->thp",
                weights,
                xs[:, part_start : part_start + group, :],
                preferred_element_type=jnp.float32,
            )
        )
    inner = jnp.concatenate(pieces, axis=1)
    carry = chain_carry(block_decay, local)
    carried = carry.astype(jnp.bfloat16)
    outer = (
        jnp.exp(cum)[:, :, None]
        * alive[:, None, None]
        * jnp.einsum("hpn,tn->thp", carried, cs, preferred_element_type=jnp.float32)
    )
    total_out = inner + outer + skip[None, :, None] * xs.astype(jnp.float32)
    normed = (
        total_out
        * lax.rsqrt(jnp.mean(total_out * total_out, axis=-1, keepdims=True) + 1e-05)
        * norm_gain.reshape(heads, head_dim)[None]
    )
    return normed.astype(jnp.bfloat16).reshape(rows, inner_width)


def solution(mesh):
    in_specs = (
        P(("dp", "ctx"), None),
        P(("dp", "ctx"), None),
        P("dp"),
        P(),
        P(),
        P(),
        P(),
        P(),
        P(),
    )
    out_specs = P(("dp", "ctx"), None)
    return jax.shard_map(body, mesh=mesh, in_specs=in_specs, out_specs=out_specs, check_vma=False)
```

```python
import jax
import jax.numpy as jnp
from jax import lax
from jax.sharding import PartitionSpec as P


def shifted(block, axis, distance):
    devices = range(lax.axis_size(axis))
    route = [(i - distance, i) for i in devices if i - distance in devices]
    return lax.ppermute(block, axis, route)


def packed(decay, local):
    lanes = local.shape[-1]
    flat = local.reshape(-1, lanes)
    spare = jnp.pad(decay, (0, 8 * lanes - decay.shape[0])).reshape(8, lanes)
    return jnp.concatenate([flat, spare], axis=0)


def unpacked(block, heads, rest):
    rows = block.shape[0] - 8
    return (block[rows, :heads], block[:rows].reshape((heads,) + rest))


def chain_carry(decay, local):
    size, position = (lax.axis_size("ctx"), lax.axis_index("ctx"))
    chips = size // 2
    core = position % 2
    low = core == 0
    heads = decay.shape[0]
    half = heads // 2
    rest = local.shape[1:]
    swap = [(2 * i + j, 2 * i + 1 - j) for i in range(chips) for j in range(2)]
    mine = lax.dynamic_slice_in_dim(local, core * half, half, 0)
    theirs = lax.dynamic_slice_in_dim(local, (1 - core) * half, half, 0)
    got = lax.ppermute(packed(decay, theirs), "ctx", swap)
    rows = half * rest[0]
    got_local = got[:rows].reshape((half,) + rest)
    got_decay = got[rows:].reshape(-1)[:heads]
    decay_hi = lax.dynamic_slice_in_dim(jnp.where(low, got_decay, decay), core * half, half, 0)
    decay_lo = lax.dynamic_slice_in_dim(jnp.where(low, decay, got_decay), core * half, half, 0)
    local_lo = jnp.where(low, mine, got_local)
    local_hi = jnp.where(low, got_local, mine)
    chip_decay = decay_hi * decay_lo
    chip_local = decay_hi[:, None, None] * local_lo + local_hi
    one = [(i, i + 2) for i in range(size - 2)]
    two = [(i, i + 4) for i in range(size - 4)]
    first_hop = lax.ppermute(packed(chip_decay, chip_local), "ctx", one)
    second_hop = lax.ppermute(first_hop, "ctx", one)
    decay_a, local_a = unpacked(first_hop, half, rest)
    decay_b, local_b = unpacked(second_hop, half, rest)
    decay_ab = decay_a * decay_b
    local_ab = decay_a[:, None, None] * local_b + local_a
    local_c = lax.ppermute(local_ab, "ctx", two)
    carry_half = decay_ab[:, None, None] * local_c + local_ab
    onward = decay_lo[:, None, None] * carry_half + local_lo
    got_end = lax.ppermute(jnp.where(low, onward, carry_half), "ctx", swap)
    first = jnp.where(low, carry_half, got_end)
    second = jnp.where(low, got_end, onward)
    return jnp.concatenate([first, second], axis=0)


def body(xbc, dt_raw, lengths, conv_weight, conv_bias, dt_bias, decay_rate, skip, norm_gain):
    rows = xbc.shape[0]
    heads = dt_raw.shape[1]
    inner_width = norm_gain.shape[0]
    head_dim = inner_width // heads
    state_dim = (xbc.shape[1] - inner_width) // 2
    taps = conv_weight.shape[0]
    device = lax.axis_index("ctx")
    first = device * rows
    ends = jnp.cumsum(lengths)
    places = first - (taps - 1) + jnp.arange(rows + taps - 1, dtype=jnp.int32)
    counted = jnp.sum((places[:, None] >= ends[None, :]).astype(jnp.int32), axis=1)
    seg_wide = jnp.where(places < 0, -1, counted)
    seg = seg_wide[taps - 1 :]
    start = seg != seg_wide[taps - 2 : -1]
    rim = shifted(xbc[rows - (taps - 1) :], "ctx", 1)
    widened = jnp.concatenate([rim, xbc], axis=0)
    total = conv_bias[None, :] + conv_weight[taps - 1][None, :] * xbc.astype(jnp.float32)
    for lag in range(1, taps):
        moved = widened[taps - 1 - lag : taps - 1 - lag + rows].astype(jnp.float32)
        same = seg_wide[taps - 1 - lag : taps - 1 - lag + rows] == seg
        total = total + conv_weight[taps - 1 - lag][None, :] * jnp.where(same[:, None], moved, 0.0)
    act = jax.nn.silu(total).astype(jnp.bfloat16)
    xs = act[:, :inner_width].reshape(rows, heads, head_dim)
    bs = act[:, inner_width : inner_width + state_dim]
    cs = act[:, inner_width + state_dim :]
    step_size = jax.nn.softplus(dt_raw + dt_bias[None, :])
    cum = jnp.cumsum(-step_size * decay_rate[None, :], axis=0)
    alive = (jnp.cumsum(start.astype(jnp.int32)) == 0).astype(jnp.float32)
    same_end = (seg == seg[-1]).astype(jnp.float32)
    factor = jnp.exp(cum[-1][None, :] - cum) * same_end[:, None] * step_size
    scaled = (factor[:, :, None] * xs.astype(jnp.float32)).astype(jnp.bfloat16)
    local = jnp.einsum("shp,sn->hpn", scaled, bs, preferred_element_type=jnp.float32)
    block_decay = jnp.exp(cum[-1]) * alive[-1]
    scores = jnp.dot(cs, bs.T, preferred_element_type=jnp.float32)
    index = jnp.arange(rows, dtype=jnp.int32)
    mask = (index[:, None] >= index[None, :]) & (seg[:, None] == seg[None, :])
    group = 8
    pieces = []
    for part_start in range(0, heads, group):
        cum_part = cum[:, part_start : part_start + group].T
        diff = cum_part[:, :, None] - cum_part[:, None, :]
        decay = jnp.where(mask[None], jnp.exp(jnp.where(mask[None], diff, 0.0)), 0.0)
        weights = (
            scores[None] * decay * step_size[:, part_start : part_start + group].T[:, None, :]
        ).astype(jnp.bfloat16)
        pieces.append(
            jnp.einsum(
                "hts,shp->thp",
                weights,
                xs[:, part_start : part_start + group, :],
                preferred_element_type=jnp.float32,
            )
        )
    inner = jnp.concatenate(pieces, axis=1)
    carry = chain_carry(block_decay, local)
    carried = carry.astype(jnp.bfloat16)
    outer = (
        jnp.exp(cum)[:, :, None]
        * alive[:, None, None]
        * jnp.einsum("hpn,tn->thp", carried, cs, preferred_element_type=jnp.float32)
    )
    total_out = inner + outer + skip[None, :, None] * xs.astype(jnp.float32)
    normed = (
        total_out
        * lax.rsqrt(jnp.mean(total_out * total_out, axis=-1, keepdims=True) + 1e-05)
        * norm_gain.reshape(heads, head_dim)[None]
    )
    return normed.astype(jnp.bfloat16).reshape(rows, inner_width)


def solution(mesh):
    in_specs = (
        P(("dp", "ctx"), None),
        P(("dp", "ctx"), None),
        P("dp"),
        P(),
        P(),
        P(),
        P(),
        P(),
        P(),
    )
    out_specs = P(("dp", "ctx"), None)
    return jax.shard_map(body, mesh=mesh, in_specs=in_specs, out_specs=out_specs, check_vma=False)
```

```python
import jax
import jax.numpy as jnp
from jax import lax
from jax.sharding import PartitionSpec as P


def shifted(block, axis, distance):
    devices = range(lax.axis_size(axis))
    route = [(i - distance, i) for i in devices if i - distance in devices]
    return lax.ppermute(block, axis, route)


def packed(decay, local):
    lanes = local.shape[-1]
    flat = local.reshape(-1, lanes)
    spare = jnp.pad(decay, (0, 8 * lanes - decay.shape[0])).reshape(8, lanes)
    return jnp.concatenate([flat, spare], axis=0)


def unpacked(block, heads, rest):
    rows = block.shape[0] - 8
    return (block[rows, :heads], block[:rows].reshape((heads,) + rest))


def chain_carry(decay, local):
    size, position = (lax.axis_size("ctx"), lax.axis_index("ctx"))
    chips = size // 2
    core = position % 2
    low = core == 0
    heads = decay.shape[0]
    half = heads // 2
    rest = local.shape[1:]
    swap = [(2 * i + j, 2 * i + 1 - j) for i in range(chips) for j in range(2)]
    mine = lax.dynamic_slice_in_dim(local, core * half, half, 0)
    theirs = lax.dynamic_slice_in_dim(local, (1 - core) * half, half, 0)
    got = lax.ppermute(packed(decay, theirs), "ctx", swap)
    rows = half * rest[0]
    got_local = got[:rows].reshape((half,) + rest)
    got_decay = got[rows:].reshape(-1)[:heads]
    decay_hi = lax.dynamic_slice_in_dim(jnp.where(low, got_decay, decay), core * half, half, 0)
    decay_lo = lax.dynamic_slice_in_dim(jnp.where(low, decay, got_decay), core * half, half, 0)
    local_lo = jnp.where(low, mine, got_local)
    local_hi = jnp.where(low, got_local, mine)
    chip_decay = decay_hi * decay_lo
    chip_local = decay_hi[:, None, None] * local_lo + local_hi
    one = [(i, i + 2) for i in range(size - 2)]
    two = [(i, i + 4) for i in range(size - 4)]
    first_hop = lax.ppermute(packed(chip_decay, chip_local), "ctx", one)
    second_hop = lax.ppermute(first_hop, "ctx", one)
    decay_a, local_a = unpacked(first_hop, half, rest)
    decay_b, local_b = unpacked(second_hop, half, rest)
    decay_ab = decay_a * decay_b
    local_ab = decay_a[:, None, None] * local_b + local_a
    local_c = lax.ppermute(local_ab.astype(jnp.bfloat16), "ctx", two).astype(jnp.float32)
    carry_half = decay_ab[:, None, None] * local_c + local_ab
    onward = decay_lo[:, None, None] * carry_half + local_lo
    got_end = lax.ppermute(jnp.where(low, onward, carry_half), "ctx", swap)
    first = jnp.where(low, carry_half, got_end)
    second = jnp.where(low, got_end, onward)
    return jnp.concatenate([first, second], axis=0)


def body(xbc, dt_raw, lengths, conv_weight, conv_bias, dt_bias, decay_rate, skip, norm_gain):
    rows = xbc.shape[0]
    heads = dt_raw.shape[1]
    inner_width = norm_gain.shape[0]
    head_dim = inner_width // heads
    state_dim = (xbc.shape[1] - inner_width) // 2
    taps = conv_weight.shape[0]
    device = lax.axis_index("ctx")
    first = device * rows
    ends = jnp.cumsum(lengths)
    places = first - (taps - 1) + jnp.arange(rows + taps - 1, dtype=jnp.int32)
    counted = jnp.sum((places[:, None] >= ends[None, :]).astype(jnp.int32), axis=1)
    seg_wide = jnp.where(places < 0, -1, counted)
    seg = seg_wide[taps - 1 :]
    start = seg != seg_wide[taps - 2 : -1]
    rim = shifted(xbc[rows - (taps - 1) :], "ctx", 1)
    widened = jnp.concatenate([rim, xbc], axis=0)
    total = conv_bias[None, :] + conv_weight[taps - 1][None, :] * xbc.astype(jnp.float32)
    for lag in range(1, taps):
        moved = widened[taps - 1 - lag : taps - 1 - lag + rows].astype(jnp.float32)
        same = seg_wide[taps - 1 - lag : taps - 1 - lag + rows] == seg
        total = total + conv_weight[taps - 1 - lag][None, :] * jnp.where(same[:, None], moved, 0.0)
    act = jax.nn.silu(total).astype(jnp.bfloat16)
    xs = act[:, :inner_width].reshape(rows, heads, head_dim)
    bs = act[:, inner_width : inner_width + state_dim]
    cs = act[:, inner_width + state_dim :]
    step_size = jax.nn.softplus(dt_raw + dt_bias[None, :])
    cum = jnp.cumsum(-step_size * decay_rate[None, :], axis=0)
    alive = (jnp.cumsum(start.astype(jnp.int32)) == 0).astype(jnp.float32)
    same_end = (seg == seg[-1]).astype(jnp.float32)
    factor = jnp.exp(cum[-1][None, :] - cum) * same_end[:, None] * step_size
    scaled = (factor[:, :, None] * xs.astype(jnp.float32)).astype(jnp.bfloat16)
    local = jnp.einsum("shp,sn->hpn", scaled, bs, preferred_element_type=jnp.float32)
    block_decay = jnp.exp(cum[-1]) * alive[-1]
    scores = jnp.dot(cs, bs.T, preferred_element_type=jnp.float32)
    index = jnp.arange(rows, dtype=jnp.int32)
    mask = (index[:, None] >= index[None, :]) & (seg[:, None] == seg[None, :])
    group = 8
    pieces = []
    for part_start in range(0, heads, group):
        cum_part = cum[:, part_start : part_start + group].T
        diff = cum_part[:, :, None] - cum_part[:, None, :]
        decay = jnp.where(mask[None], jnp.exp(jnp.where(mask[None], diff, 0.0)), 0.0)
        weights = (
            scores[None] * decay * step_size[:, part_start : part_start + group].T[:, None, :]
        ).astype(jnp.bfloat16)
        pieces.append(
            jnp.einsum(
                "hts,shp->thp",
                weights,
                xs[:, part_start : part_start + group, :],
                preferred_element_type=jnp.float32,
            )
        )
    inner = jnp.concatenate(pieces, axis=1)
    carry = chain_carry(block_decay, local)
    carried = carry.astype(jnp.bfloat16)
    outer = (
        jnp.exp(cum)[:, :, None]
        * alive[:, None, None]
        * jnp.einsum("hpn,tn->thp", carried, cs, preferred_element_type=jnp.float32)
    )
    total_out = inner + outer + skip[None, :, None] * xs.astype(jnp.float32)
    normed = (
        total_out
        * lax.rsqrt(jnp.mean(total_out * total_out, axis=-1, keepdims=True) + 1e-05)
        * norm_gain.reshape(heads, head_dim)[None]
    )
    return normed.astype(jnp.bfloat16).reshape(rows, inner_width)


def solution(mesh):
    in_specs = (
        P(("dp", "ctx"), None),
        P(("dp", "ctx"), None),
        P("dp"),
        P(),
        P(),
        P(),
        P(),
        P(),
        P(),
    )
    out_specs = P(("dp", "ctx"), None)
    return jax.shard_map(body, mesh=mesh, in_specs=in_specs, out_specs=out_specs, check_vma=False)
```

```python
import jax
import jax.numpy as jnp
from jax import lax
from jax.sharding import PartitionSpec as P


def shifted(block, axis, distance):
    devices = range(lax.axis_size(axis))
    route = [(i - distance, i) for i in devices if i - distance in devices]
    return lax.ppermute(block, axis, route)


def packed(decay, local):
    lanes = local.shape[-1]
    flat = local.reshape(-1, lanes)
    spare = jnp.pad(decay, (0, 8 * lanes - decay.shape[0])).reshape(8, lanes)
    return jnp.concatenate([flat, spare], axis=0)


def unpacked(block, heads, rest):
    rows = block.shape[0] - 8
    return (block[rows, :heads], block[:rows].reshape((heads,) + rest))


def chain_carry(decay, local):
    size, position = (lax.axis_size("ctx"), lax.axis_index("ctx"))
    chips = size // 2
    core = position % 2
    low = core == 0
    heads = decay.shape[0]
    half = heads // 2
    rest = local.shape[1:]
    swap = [(2 * i + j, 2 * i + 1 - j) for i in range(chips) for j in range(2)]
    mine = lax.dynamic_slice_in_dim(local, core * half, half, 0)
    theirs = lax.dynamic_slice_in_dim(local, (1 - core) * half, half, 0)
    got = lax.ppermute(packed(decay, theirs), "ctx", swap)
    rows = half * rest[0]
    got_local = got[:rows].reshape((half,) + rest)
    got_decay = got[rows:].reshape(-1)[:heads]
    decay_hi = lax.dynamic_slice_in_dim(jnp.where(low, got_decay, decay), core * half, half, 0)
    decay_lo = lax.dynamic_slice_in_dim(jnp.where(low, decay, got_decay), core * half, half, 0)
    local_lo = jnp.where(low, mine, got_local)
    local_hi = jnp.where(low, got_local, mine)
    chip_decay = decay_hi * decay_lo
    chip_local = decay_hi[:, None, None] * local_lo + local_hi
    one = [(i, i + 2) for i in range(size - 2)]
    two = [(i, i + 4) for i in range(size - 4)]
    first_hop = lax.ppermute(packed(chip_decay, chip_local), "ctx", one)
    decay_a, local_a = unpacked(first_hop, half, rest)
    decay_b, local_b = unpacked(lax.ppermute(first_hop.astype(jnp.bfloat16), "ctx", one).astype(jnp.float32), half, rest)
    decay_ab = decay_a * decay_b
    local_ab = decay_a[:, None, None] * local_b + local_a
    local_c = lax.ppermute(local_ab.astype(jnp.bfloat16), "ctx", two).astype(jnp.float32)
    carry_half = decay_ab[:, None, None] * local_c + local_ab
    onward = decay_lo[:, None, None] * carry_half + local_lo
    got_end = lax.ppermute(jnp.where(low, onward, carry_half), "ctx", swap)
    first = jnp.where(low, carry_half, got_end)
    second = jnp.where(low, got_end, onward)
    return jnp.concatenate([first, second], axis=0)


def body(xbc, dt_raw, lengths, conv_weight, conv_bias, dt_bias, decay_rate, skip, norm_gain):
    rows = xbc.shape[0]
    heads = dt_raw.shape[1]
    inner_width = norm_gain.shape[0]
    head_dim = inner_width // heads
    state_dim = (xbc.shape[1] - inner_width) // 2
    taps = conv_weight.shape[0]
    device = lax.axis_index("ctx")
    first = device * rows
    ends = jnp.cumsum(lengths)
    places = first - (taps - 1) + jnp.arange(rows + taps - 1, dtype=jnp.int32)
    counted = jnp.sum((places[:, None] >= ends[None, :]).astype(jnp.int32), axis=1)
    seg_wide = jnp.where(places < 0, -1, counted)
    seg = seg_wide[taps - 1 :]
    start = seg != seg_wide[taps - 2 : -1]
    rim = shifted(xbc[rows - (taps - 1) :], "ctx", 1)
    widened = jnp.concatenate([rim, xbc], axis=0)
    total = conv_bias[None, :] + conv_weight[taps - 1][None, :] * xbc.astype(jnp.float32)
    for lag in range(1, taps):
        moved = widened[taps - 1 - lag : taps - 1 - lag + rows].astype(jnp.float32)
        same = seg_wide[taps - 1 - lag : taps - 1 - lag + rows] == seg
        total = total + conv_weight[taps - 1 - lag][None, :] * jnp.where(same[:, None], moved, 0.0)
    act = jax.nn.silu(total).astype(jnp.bfloat16)
    xs = act[:, :inner_width].reshape(rows, heads, head_dim)
    bs = act[:, inner_width : inner_width + state_dim]
    cs = act[:, inner_width + state_dim :]
    step_size = jax.nn.softplus(dt_raw + dt_bias[None, :])
    cum = jnp.cumsum(-step_size * decay_rate[None, :], axis=0)
    alive = (jnp.cumsum(start.astype(jnp.int32)) == 0).astype(jnp.float32)
    same_end = (seg == seg[-1]).astype(jnp.float32)
    factor = jnp.exp(cum[-1][None, :] - cum) * same_end[:, None] * step_size
    scaled = (factor[:, :, None] * xs.astype(jnp.float32)).astype(jnp.bfloat16)
    local = jnp.einsum("shp,sn->hpn", scaled, bs, preferred_element_type=jnp.float32)
    block_decay = jnp.exp(cum[-1]) * alive[-1]
    scores = jnp.dot(cs, bs.T, preferred_element_type=jnp.float32)
    index = jnp.arange(rows, dtype=jnp.int32)
    mask = (index[:, None] >= index[None, :]) & (seg[:, None] == seg[None, :])
    group = 8
    pieces = []
    for part_start in range(0, heads, group):
        cum_part = cum[:, part_start : part_start + group].T
        diff = cum_part[:, :, None] - cum_part[:, None, :]
        decay = jnp.where(mask[None], jnp.exp(jnp.where(mask[None], diff, 0.0)), 0.0)
        weights = (
            scores[None] * decay * step_size[:, part_start : part_start + group].T[:, None, :]
        ).astype(jnp.bfloat16)
        pieces.append(
            jnp.einsum(
                "hts,shp->thp",
                weights,
                xs[:, part_start : part_start + group, :],
                preferred_element_type=jnp.float32,
            )
        )
    inner = jnp.concatenate(pieces, axis=1)
    carry = chain_carry(block_decay, local)
    carried = carry.astype(jnp.bfloat16)
    outer = (
        jnp.exp(cum)[:, :, None]
        * alive[:, None, None]
        * jnp.einsum("hpn,tn->thp", carried, cs, preferred_element_type=jnp.float32)
    )
    total_out = inner + outer + skip[None, :, None] * xs.astype(jnp.float32)
    normed = (
        total_out
        * lax.rsqrt(jnp.mean(total_out * total_out, axis=-1, keepdims=True) + 1e-05)
        * norm_gain.reshape(heads, head_dim)[None]
    )
    return normed.astype(jnp.bfloat16).reshape(rows, inner_width)


def solution(mesh):
    in_specs = (
        P(("dp", "ctx"), None),
        P(("dp", "ctx"), None),
        P("dp"),
        P(),
        P(),
        P(),
        P(),
        P(),
        P(),
    )
    out_specs = P(("dp", "ctx"), None)
    return jax.shard_map(body, mesh=mesh, in_specs=in_specs, out_specs=out_specs, check_vma=False)
```

```python
import jax
import jax.numpy as jnp
from jax import lax
from jax.sharding import PartitionSpec as P


def shifted(block, axis, distance):
    devices = range(lax.axis_size(axis))
    route = [(i - distance, i) for i in devices if i - distance in devices]
    return lax.ppermute(block, axis, route)


def packed(decay, local):
    lanes = local.shape[-1]
    flat = local.reshape(-1, lanes)
    spare = jnp.pad(decay, (0, 8 * lanes - decay.shape[0])).reshape(8, lanes)
    return jnp.concatenate([flat, spare], axis=0)


def unpacked(block, heads, rest):
    rows = block.shape[0] - 8
    return (block[rows, :heads], block[:rows].reshape((heads,) + rest))


def chain_carry(decay, local):
    size, position = (lax.axis_size("ctx"), lax.axis_index("ctx"))
    chips = size // 2
    core = position % 2
    low = core == 0
    heads = decay.shape[0]
    half = heads // 2
    rest = local.shape[1:]
    swap = [(2 * i + j, 2 * i + 1 - j) for i in range(chips) for j in range(2)]
    mine = lax.dynamic_slice_in_dim(local, core * half, half, 0)
    theirs = lax.dynamic_slice_in_dim(local, (1 - core) * half, half, 0)
    got = lax.ppermute(packed(decay, theirs), "ctx", swap)
    rows = half * rest[0]
    got_local = got[:rows].reshape((half,) + rest)
    got_decay = got[rows:].reshape(-1)[:heads]
    decay_hi = lax.dynamic_slice_in_dim(jnp.where(low, got_decay, decay), core * half, half, 0)
    decay_lo = lax.dynamic_slice_in_dim(jnp.where(low, decay, got_decay), core * half, half, 0)
    local_lo = jnp.where(low, mine, got_local)
    local_hi = jnp.where(low, got_local, mine)
    chip_decay = decay_hi * decay_lo
    chip_local = decay_hi[:, None, None] * local_lo + local_hi
    one = [(i, i + 2) for i in range(size - 2)]
    two = [(i, i + 4) for i in range(size - 4)]
    first_hop = lax.ppermute(packed(chip_decay, chip_local), "ctx", one)
    decay_a, local_a = unpacked(first_hop, half, rest)
    decay_b, local_b = unpacked(lax.ppermute(first_hop.astype(jnp.bfloat16), "ctx", one).astype(jnp.float32), half, rest)
    decay_ab = decay_a * decay_b
    local_ab = decay_a[:, None, None] * local_b + local_a
    local_c = lax.ppermute(local_ab.astype(jnp.bfloat16), "ctx", two).astype(jnp.float32)
    carry_half = decay_ab[:, None, None] * local_c + local_ab
    onward = decay_lo[:, None, None] * carry_half + local_lo
    got_end = lax.ppermute(jnp.where(low, onward, carry_half), "ctx", swap)
    first = jnp.where(low, carry_half, got_end)
    second = jnp.where(low, got_end, onward)
    return jnp.concatenate([first, second], axis=0)


def body(xbc, dt_raw, lengths, conv_weight, conv_bias, dt_bias, decay_rate, skip, norm_gain):
    rows = xbc.shape[0]
    heads = dt_raw.shape[1]
    inner_width = norm_gain.shape[0]
    head_dim = inner_width // heads
    state_dim = (xbc.shape[1] - inner_width) // 2
    taps = conv_weight.shape[0]
    device = lax.axis_index("ctx")
    first = device * rows
    docs = lengths.shape[0]
    order = jnp.arange(docs, dtype=jnp.int32)
    ends = jnp.sum(jnp.where(order[None, :] <= order[:, None], lengths[None, :], 0), axis=1)
    halo = 16
    places = first - halo + jnp.arange(rows + halo, dtype=jnp.int32)
    counted = jnp.sum((places[:, None] >= ends[None, :]).astype(jnp.int32), axis=1)
    seg_wide = jnp.where(places < 0, -1, counted)
    seg = seg_wide[halo:]
    rim = shifted(xbc[rows - halo :], "ctx", 1)
    widened = jnp.concatenate([rim, xbc], axis=0)
    total = conv_bias[None, :] + conv_weight[taps - 1][None, :] * xbc.astype(jnp.float32)
    for lag in range(1, taps):
        moved = widened[halo - lag : halo - lag + rows].astype(jnp.float32)
        same = seg_wide[halo - lag : halo - lag + rows] == seg
        total = total + conv_weight[taps - 1 - lag][None, :] * jnp.where(same[:, None], moved, 0.0)
    act = jax.nn.silu(total).astype(jnp.bfloat16)
    xs = act[:, :inner_width].reshape(rows, heads, head_dim)
    bs = act[:, inner_width : inner_width + state_dim]
    cs = act[:, inner_width + state_dim :]
    step_size = jax.nn.softplus(dt_raw + dt_bias[None, :])
    cum = jnp.cumsum(-step_size * decay_rate[None, :], axis=0)
    alive = (seg == seg_wide[halo - 1]).astype(jnp.float32)
    same_end = (seg == seg[-1]).astype(jnp.float32)
    factor = jnp.exp(cum[-1][None, :] - cum) * same_end[:, None] * step_size
    scaled = (factor[:, :, None] * xs.astype(jnp.float32)).astype(jnp.bfloat16)
    local = jnp.einsum("shp,sn->hpn", scaled, bs, preferred_element_type=jnp.float32)
    block_decay = jnp.exp(cum[-1]) * alive[-1]
    scores = jnp.dot(cs, bs.T, preferred_element_type=jnp.float32)
    index = jnp.arange(rows, dtype=jnp.int32)
    mask = (index[:, None] >= index[None, :]) & (seg[:, None] == seg[None, :])
    group = 8
    pieces = []
    for part_start in range(0, heads, group):
        cum_part = cum[:, part_start : part_start + group].T
        diff = cum_part[:, :, None] - cum_part[:, None, :]
        decay = jnp.where(mask[None], jnp.exp(jnp.where(mask[None], diff, 0.0)), 0.0)
        weights = (
            scores[None] * decay * step_size[:, part_start : part_start + group].T[:, None, :]
        ).astype(jnp.bfloat16)
        pieces.append(
            jnp.einsum(
                "hts,shp->thp",
                weights,
                xs[:, part_start : part_start + group, :],
                preferred_element_type=jnp.float32,
            )
        )
    inner = jnp.concatenate(pieces, axis=1)
    carry = chain_carry(block_decay, local)
    carried = carry.astype(jnp.bfloat16)
    outer = (
        jnp.exp(cum)[:, :, None]
        * alive[:, None, None]
        * jnp.einsum("hpn,tn->thp", carried, cs, preferred_element_type=jnp.float32)
    )
    total_out = inner + outer + skip[None, :, None] * xs.astype(jnp.float32)
    normed = (
        total_out
        * lax.rsqrt(jnp.mean(total_out * total_out, axis=-1, keepdims=True) + 1e-05)
        * norm_gain.reshape(heads, head_dim)[None]
    )
    return normed.astype(jnp.bfloat16).reshape(rows, inner_width)


def solution(mesh):
    in_specs = (
        P(("dp", "ctx"), None),
        P(("dp", "ctx"), None),
        P("dp"),
        P(),
        P(),
        P(),
        P(),
        P(),
        P(),
    )
    out_specs = P(("dp", "ctx"), None)
    return jax.shard_map(body, mesh=mesh, in_specs=in_specs, out_specs=out_specs, check_vma=False)
```

```python
import jax
import jax.numpy as jnp
from jax import lax
from jax.sharding import PartitionSpec as P


def shifted(block, axis, distance):
    devices = range(lax.axis_size(axis))
    route = [(i - distance, i) for i in devices if i - distance in devices]
    return lax.ppermute(block, axis, route)


def packed(decay, local):
    lanes = local.shape[-1]
    flat = local.reshape(-1, lanes)
    spare = jnp.pad(decay, (0, 8 * lanes - decay.shape[0])).reshape(8, lanes)
    return jnp.concatenate([flat, spare], axis=0)


def unpacked(block, heads, rest):
    rows = block.shape[0] - 8
    return (block[rows, :heads], block[:rows].reshape((heads,) + rest))


def chain_carry(decay, local, held):
    size, position = (lax.axis_size("ctx"), lax.axis_index("ctx"))
    chips = size // 2
    core = position % 2
    low = core == 0
    heads = decay.shape[0]
    half = heads // 2
    rest = local.shape[1:]
    swap = [(2 * i + j, 2 * i + 1 - j) for i in range(chips) for j in range(2)]
    mine = lax.dynamic_slice_in_dim(local, core * half, half, 0)
    theirs = lax.dynamic_slice_in_dim(local, (1 - core) * half, half, 0)
    got = lax.ppermute(packed(decay, theirs), "ctx", swap)
    rows = half * rest[0]
    got_local = got[:rows].reshape((half,) + rest)
    got_decay = got[rows:].reshape(-1)[:heads]
    decay_hi = lax.dynamic_slice_in_dim(jnp.where(low, got_decay, decay), core * half, half, 0)
    decay_lo = lax.dynamic_slice_in_dim(jnp.where(low, decay, got_decay), core * half, half, 0)
    local_lo = jnp.where(low, mine, got_local)
    local_hi = jnp.where(low, got_local, mine)
    chip_decay = decay_hi * decay_lo
    chip_local = decay_hi[:, None, None] * local_lo + local_hi
    one = [(i, i + 2) for i in range(size - 2)]
    two = [(i, i + 4) for i in range(size - 4)]
    sent, held = lax.optimization_barrier((packed(chip_decay, chip_local), held))
    first_hop = lax.ppermute(sent, "ctx", one)
    decay_a, local_a = unpacked(first_hop, half, rest)
    decay_b, local_b = unpacked(lax.ppermute(first_hop.astype(jnp.bfloat16), "ctx", one).astype(jnp.float32), half, rest)
    decay_ab = decay_a * decay_b
    local_ab = decay_a[:, None, None] * local_b + local_a
    local_c = lax.ppermute(local_ab.astype(jnp.bfloat16), "ctx", two).astype(jnp.float32)
    carry_half = decay_ab[:, None, None] * local_c + local_ab
    onward = decay_lo[:, None, None] * carry_half + local_lo
    got_end = lax.ppermute(jnp.where(low, onward, carry_half), "ctx", swap)
    first = jnp.where(low, carry_half, got_end)
    second = jnp.where(low, got_end, onward)
    return (jnp.concatenate([first, second], axis=0), held)


def body(xbc, dt_raw, lengths, conv_weight, conv_bias, dt_bias, decay_rate, skip, norm_gain):
    rows = xbc.shape[0]
    heads = dt_raw.shape[1]
    inner_width = norm_gain.shape[0]
    head_dim = inner_width // heads
    state_dim = (xbc.shape[1] - inner_width) // 2
    taps = conv_weight.shape[0]
    device = lax.axis_index("ctx")
    first = device * rows
    docs = lengths.shape[0]
    order = jnp.arange(docs, dtype=jnp.int32)
    ends = jnp.sum(jnp.where(order[None, :] <= order[:, None], lengths[None, :], 0), axis=1)
    halo = 16
    places = first - halo + jnp.arange(rows + halo, dtype=jnp.int32)
    counted = jnp.sum((places[:, None] >= ends[None, :]).astype(jnp.int32), axis=1)
    seg_wide = jnp.where(places < 0, -1, counted)
    seg = seg_wide[halo:]
    rim = shifted(xbc[rows - halo :], "ctx", 1)
    widened = jnp.concatenate([rim, xbc], axis=0)
    total = conv_bias[None, :] + conv_weight[taps - 1][None, :] * xbc.astype(jnp.float32)
    for lag in range(1, taps):
        moved = widened[halo - lag : halo - lag + rows].astype(jnp.float32)
        same = seg_wide[halo - lag : halo - lag + rows] == seg
        total = total + conv_weight[taps - 1 - lag][None, :] * jnp.where(same[:, None], moved, 0.0)
    act = jax.nn.silu(total).astype(jnp.bfloat16)
    xs = act[:, :inner_width].reshape(rows, heads, head_dim)
    bs = act[:, inner_width : inner_width + state_dim]
    cs = act[:, inner_width + state_dim :]
    step_size = jax.nn.softplus(dt_raw + dt_bias[None, :])
    cum = jnp.cumsum(-step_size * decay_rate[None, :], axis=0)
    alive = (seg == seg_wide[halo - 1]).astype(jnp.float32)
    same_end = (seg == seg[-1]).astype(jnp.float32)
    factor = jnp.exp(cum[-1][None, :] - cum) * same_end[:, None] * step_size
    scaled = (factor[:, :, None] * xs.astype(jnp.float32)).astype(jnp.bfloat16)
    local = jnp.einsum("shp,sn->hpn", scaled, bs, preferred_element_type=jnp.float32)
    block_decay = jnp.exp(cum[-1]) * alive[-1]
    carry, (cum_late, step_late, seg_late) = chain_carry(block_decay, local, (cum, step_size, seg))
    scores = jnp.dot(cs, bs.T, preferred_element_type=jnp.float32)
    index = jnp.arange(rows, dtype=jnp.int32)
    mask = (index[:, None] >= index[None, :]) & (seg_late[:, None] == seg_late[None, :])
    group = 8
    pieces = []
    for part_start in range(0, heads, group):
        cum_part = cum_late[:, part_start : part_start + group].T
        diff = cum_part[:, :, None] - cum_part[:, None, :]
        decay = jnp.where(mask[None], jnp.exp(jnp.where(mask[None], diff, 0.0)), 0.0)
        weights = (
            scores[None] * decay * step_late[:, part_start : part_start + group].T[:, None, :]
        ).astype(jnp.bfloat16)
        pieces.append(
            jnp.einsum(
                "hts,shp->thp",
                weights,
                xs[:, part_start : part_start + group, :],
                preferred_element_type=jnp.float32,
            )
        )
    inner = jnp.concatenate(pieces, axis=1)
    carried = carry.astype(jnp.bfloat16)
    outer = (
        jnp.exp(cum)[:, :, None]
        * alive[:, None, None]
        * jnp.einsum("hpn,tn->thp", carried, cs, preferred_element_type=jnp.float32)
    )
    total_out = inner + outer + skip[None, :, None] * xs.astype(jnp.float32)
    normed = (
        total_out
        * lax.rsqrt(jnp.mean(total_out * total_out, axis=-1, keepdims=True) + 1e-05)
        * norm_gain.reshape(heads, head_dim)[None]
    )
    return normed.astype(jnp.bfloat16).reshape(rows, inner_width)


def solution(mesh):
    in_specs = (
        P(("dp", "ctx"), None),
        P(("dp", "ctx"), None),
        P("dp"),
        P(),
        P(),
        P(),
        P(),
        P(),
        P(),
    )
    out_specs = P(("dp", "ctx"), None)
    return jax.shard_map(body, mesh=mesh, in_specs=in_specs, out_specs=out_specs, check_vma=False)
```

```python
import jax
import jax.numpy as jnp
from jax import lax
from jax.sharding import PartitionSpec as P


def shifted(block, axis, distance):
    devices = range(lax.axis_size(axis))
    route = [(i - distance, i) for i in devices if i - distance in devices]
    return lax.ppermute(block, axis, route)


def packed(decay, local):
    lanes = local.shape[-1]
    flat = local.reshape(-1, lanes)
    spare = jnp.pad(decay, (0, 16 * lanes - decay.shape[0])).reshape(16, lanes)
    return jnp.concatenate([flat, spare], axis=0)


def unpacked(block, heads, rest):
    rows = block.shape[0] - 16
    return (block[rows, :heads], block[:rows].reshape((heads,) + rest))


def chain_carry(decay, local, held):
    size, position = (lax.axis_size("ctx"), lax.axis_index("ctx"))
    chips = size // 2
    core = position % 2
    low = core == 0
    heads = decay.shape[0]
    half = heads // 2
    rest = local.shape[1:]
    swap = [(2 * i + j, 2 * i + 1 - j) for i in range(chips) for j in range(2)]
    mine = lax.dynamic_slice_in_dim(local, core * half, half, 0)
    theirs = lax.dynamic_slice_in_dim(local, (1 - core) * half, half, 0)
    got = lax.ppermute(packed(decay, theirs), "ctx", swap)
    rows = half * rest[0]
    got_local = got[:rows].reshape((half,) + rest)
    got_decay = got[rows:].reshape(-1)[:heads]
    decay_hi = lax.dynamic_slice_in_dim(jnp.where(low, got_decay, decay), core * half, half, 0)
    decay_lo = lax.dynamic_slice_in_dim(jnp.where(low, decay, got_decay), core * half, half, 0)
    local_lo = jnp.where(low, mine, got_local)
    local_hi = jnp.where(low, got_local, mine)
    chip_decay = decay_hi * decay_lo
    chip_local = decay_hi[:, None, None] * local_lo + local_hi
    one = [(i, i + 2) for i in range(size - 2)]
    two = [(i, i + 4) for i in range(size - 4)]
    sent, held = lax.optimization_barrier((packed(chip_decay, chip_local), held))
    first_hop = lax.ppermute(sent, "ctx", one)
    decay_a, local_a = unpacked(first_hop, half, rest)
    decay_b, local_b = unpacked(lax.ppermute(first_hop.astype(jnp.bfloat16), "ctx", one).astype(jnp.float32), half, rest)
    decay_ab = decay_a * decay_b
    local_ab = decay_a[:, None, None] * local_b + local_a
    local_c = lax.ppermute(local_ab.astype(jnp.bfloat16), "ctx", two).astype(jnp.float32)
    carry_half = decay_ab[:, None, None] * local_c + local_ab
    onward = decay_lo[:, None, None] * carry_half + local_lo
    got_end = lax.ppermute(jnp.where(low, onward, carry_half), "ctx", swap)
    first = jnp.where(low, carry_half, got_end)
    second = jnp.where(low, got_end, onward)
    return (jnp.concatenate([first, second], axis=0), held)


def body(xbc, dt_raw, lengths, conv_weight, conv_bias, dt_bias, decay_rate, skip, norm_gain):
    rows = xbc.shape[0]
    heads = dt_raw.shape[1]
    inner_width = norm_gain.shape[0]
    head_dim = inner_width // heads
    state_dim = (xbc.shape[1] - inner_width) // 2
    taps = conv_weight.shape[0]
    device = lax.axis_index("ctx")
    first = device * rows
    docs = lengths.shape[0]
    order = jnp.arange(docs, dtype=jnp.int32)
    ends = jnp.sum(jnp.where(order[None, :] <= order[:, None], lengths[None, :], 0), axis=1)
    halo = 16
    places = first - halo + jnp.arange(rows + halo, dtype=jnp.int32)
    counted = jnp.sum((places[:, None] >= ends[None, :]).astype(jnp.int32), axis=1)
    seg_wide = jnp.where(places < 0, -1, counted)
    seg = seg_wide[halo:]
    rim = shifted(xbc[rows - halo :], "ctx", 1)
    widened = jnp.concatenate([rim, xbc], axis=0)
    total = conv_bias[None, :] + conv_weight[taps - 1][None, :] * xbc.astype(jnp.float32)
    for lag in range(1, taps):
        moved = widened[halo - lag : halo - lag + rows].astype(jnp.float32)
        same = seg_wide[halo - lag : halo - lag + rows] == seg
        total = total + conv_weight[taps - 1 - lag][None, :] * jnp.where(same[:, None], moved, 0.0)
    act = jax.nn.silu(total).astype(jnp.bfloat16)
    xs = act[:, :inner_width].reshape(rows, heads, head_dim)
    bs = act[:, inner_width : inner_width + state_dim]
    cs = act[:, inner_width + state_dim :]
    step_size = jax.nn.softplus(dt_raw + dt_bias[None, :])
    cum = jnp.cumsum(-step_size * decay_rate[None, :], axis=0)
    alive = (seg == seg_wide[halo - 1]).astype(jnp.float32)
    same_end = (seg == seg[-1]).astype(jnp.float32)
    factor = jnp.exp(cum[-1][None, :] - cum) * same_end[:, None] * step_size
    scaled = (factor[:, :, None] * xs.astype(jnp.float32)).astype(jnp.bfloat16)
    local = jnp.einsum("shp,sn->hpn", scaled, bs, preferred_element_type=jnp.float32)
    block_decay = jnp.exp(cum[-1]) * alive[-1]
    carry, (cum_late, step_late, seg_late, cs_late, bs_late, xs_late) = chain_carry(
        block_decay, local, (cum, step_size, seg, cs, bs, xs)
    )
    scores = jnp.dot(cs_late, bs_late.T, preferred_element_type=jnp.float32)
    index = jnp.arange(rows, dtype=jnp.int32)
    mask = (index[:, None] >= index[None, :]) & (seg_late[:, None] == seg_late[None, :])
    group = 8
    pieces = []
    for part_start in range(0, heads, group):
        cum_part = cum_late[:, part_start : part_start + group].T
        diff = cum_part[:, :, None] - cum_part[:, None, :]
        decay = jnp.where(mask[None], jnp.exp(jnp.where(mask[None], diff, 0.0)), 0.0)
        weights = (
            scores[None] * decay * step_late[:, part_start : part_start + group].T[:, None, :]
        ).astype(jnp.bfloat16)
        pieces.append(
            jnp.einsum(
                "hts,shp->thp",
                weights,
                xs_late[:, part_start : part_start + group, :],
                preferred_element_type=jnp.float32,
            )
        )
    inner = jnp.concatenate(pieces, axis=1)
    carried = carry.astype(jnp.bfloat16)
    outer = (
        jnp.exp(cum)[:, :, None]
        * alive[:, None, None]
        * jnp.einsum("hpn,tn->thp", carried, cs, preferred_element_type=jnp.float32)
    )
    total_out = inner + outer + skip[None, :, None] * xs.astype(jnp.float32)
    normed = (
        total_out
        * lax.rsqrt(jnp.mean(total_out * total_out, axis=-1, keepdims=True) + 1e-05)
        * norm_gain.reshape(heads, head_dim)[None]
    )
    return normed.astype(jnp.bfloat16).reshape(rows, inner_width)


def solution(mesh):
    in_specs = (
        P(("dp", "ctx"), None),
        P(("dp", "ctx"), None),
        P("dp"),
        P(),
        P(),
        P(),
        P(),
        P(),
        P(),
    )
    out_specs = P(("dp", "ctx"), None)
    return jax.shard_map(body, mesh=mesh, in_specs=in_specs, out_specs=out_specs, check_vma=False)
```

```python
import jax
import jax.numpy as jnp
from jax import lax
from jax.sharding import PartitionSpec as P


def shifted(block, axis, distance):
    devices = range(lax.axis_size(axis))
    route = [(i - distance, i) for i in devices if i - distance in devices]
    return lax.ppermute(block, axis, route)


def packed(decay, local):
    lanes = local.shape[-1]
    flat = local.reshape(-1, lanes)
    spare = jnp.pad(decay, (0, 8 * lanes - decay.shape[0])).reshape(8, lanes)
    return jnp.concatenate([flat, spare], axis=0)


def unpacked(block, heads, rest):
    rows = block.shape[0] - 8
    return (block[rows, :heads], block[:rows].reshape((heads,) + rest))


def chain_carry(decay, scaled, bs, held):
    size, position = (lax.axis_size("ctx"), lax.axis_index("ctx"))
    chips = size // 2
    core = position % 2
    low = core == 0
    heads = decay.shape[0]
    half = heads // 2
    rows = scaled.shape[0]
    width = half * scaled.shape[2]
    swap = [(2 * i + j, 2 * i + 1 - j) for i in range(chips) for j in range(2)]
    front, back = scaled[:, :half], scaled[:, half:]
    mine_x = jnp.where(low, front, back)
    theirs_x = jnp.where(low, back, front)
    mine = jnp.einsum("shp,sn->hpn", mine_x, bs, preferred_element_type=jnp.float32)
    rest = mine.shape[1:]
    top = decay.astype(jnp.bfloat16)
    middle = (decay - top.astype(jnp.float32)).astype(jnp.bfloat16)
    bottom = (decay - top.astype(jnp.float32) - middle.astype(jnp.float32)).astype(jnp.bfloat16)
    pieces = jnp.zeros((rows, bs.shape[1]), jnp.bfloat16).at[:3, :heads].set(jnp.stack([top, middle, bottom]))
    got = lax.ppermute(
        jnp.concatenate([theirs_x.reshape(rows, width), bs, pieces], axis=1), "ctx", swap
    )
    got_x = got[:, :width].reshape(scaled.shape[0], half, scaled.shape[2])
    got_b = got[:, width : width + bs.shape[1]]
    spare = got[:3, width + bs.shape[1] : width + bs.shape[1] + heads].astype(jnp.float32)
    got_decay = (spare[0] + spare[1]) + spare[2]
    got_local = jnp.einsum("shp,sn->hpn", got_x, got_b, preferred_element_type=jnp.float32)
    decay_hi = lax.dynamic_slice_in_dim(jnp.where(low, got_decay, decay), core * half, half, 0)
    decay_lo = lax.dynamic_slice_in_dim(jnp.where(low, decay, got_decay), core * half, half, 0)
    local_lo = jnp.where(low, mine, got_local)
    local_hi = jnp.where(low, got_local, mine)
    chip_decay = decay_hi * decay_lo
    chip_local = decay_hi[:, None, None] * local_lo + local_hi
    one = [(i, i + 2) for i in range(size - 2)]
    two = [(i, i + 4) for i in range(size - 4)]
    sent, held = lax.optimization_barrier((packed(chip_decay, chip_local), held))
    first_hop = lax.ppermute(sent, "ctx", one)
    decay_a, local_a = unpacked(first_hop, half, rest)
    decay_b, local_b = unpacked(lax.ppermute(first_hop.astype(jnp.bfloat16), "ctx", one).astype(jnp.float32), half, rest)
    decay_ab = decay_a * decay_b
    local_ab = decay_a[:, None, None] * local_b + local_a
    local_c = lax.ppermute(local_ab.astype(jnp.bfloat16), "ctx", two).astype(jnp.float32)
    carry_half = decay_ab[:, None, None] * local_c + local_ab
    onward = decay_lo[:, None, None] * carry_half + local_lo
    got_end = lax.ppermute(jnp.where(low, onward, carry_half), "ctx", swap)
    first = jnp.where(low, carry_half, got_end)
    second = jnp.where(low, got_end, onward)
    return (jnp.concatenate([first, second], axis=0), held)


def body(xbc, dt_raw, lengths, conv_weight, conv_bias, dt_bias, decay_rate, skip, norm_gain):
    rows = xbc.shape[0]
    heads = dt_raw.shape[1]
    inner_width = norm_gain.shape[0]
    head_dim = inner_width // heads
    state_dim = (xbc.shape[1] - inner_width) // 2
    taps = conv_weight.shape[0]
    device = lax.axis_index("ctx")
    first = device * rows
    docs = lengths.shape[0]
    order = jnp.arange(docs, dtype=jnp.int32)
    ends = jnp.sum(jnp.where(order[None, :] <= order[:, None], lengths[None, :], 0), axis=1)
    halo = 16
    places = first - halo + jnp.arange(rows + halo, dtype=jnp.int32)
    counted = jnp.sum((places[:, None] >= ends[None, :]).astype(jnp.int32), axis=1)
    seg_wide = jnp.where(places < 0, -1, counted)
    seg = seg_wide[halo:]
    rim = shifted(xbc[rows - halo :], "ctx", 1)
    widened = jnp.concatenate([rim, xbc], axis=0)
    total = conv_bias[None, :] + conv_weight[taps - 1][None, :] * xbc.astype(jnp.float32)
    for lag in range(1, taps):
        moved = widened[halo - lag : halo - lag + rows].astype(jnp.float32)
        same = seg_wide[halo - lag : halo - lag + rows] == seg
        total = total + conv_weight[taps - 1 - lag][None, :] * jnp.where(same[:, None], moved, 0.0)
    act = jax.nn.silu(total).astype(jnp.bfloat16)
    xs = act[:, :inner_width].reshape(rows, heads, head_dim)
    bs = act[:, inner_width : inner_width + state_dim]
    cs = act[:, inner_width + state_dim :]
    step_size = jax.nn.softplus(dt_raw + dt_bias[None, :])
    cum = jnp.cumsum(-step_size * decay_rate[None, :], axis=0)
    alive = (seg == seg_wide[halo - 1]).astype(jnp.float32)
    same_end = (seg == seg[-1]).astype(jnp.float32)
    factor = jnp.exp(cum[-1][None, :] - cum) * same_end[:, None] * step_size
    scaled = (factor[:, :, None] * xs.astype(jnp.float32)).astype(jnp.bfloat16)
    block_decay = jnp.exp(cum[-1]) * alive[-1]
    carry, (cum_late, step_late, seg_late) = chain_carry(block_decay, scaled, bs, (cum, step_size, seg))
    scores = jnp.dot(cs, bs.T, preferred_element_type=jnp.float32)
    index = jnp.arange(rows, dtype=jnp.int32)
    mask = (index[:, None] >= index[None, :]) & (seg_late[:, None] == seg_late[None, :])
    group = 8
    pieces = []
    for part_start in range(0, heads, group):
        cum_part = cum_late[:, part_start : part_start + group].T
        diff = cum_part[:, :, None] - cum_part[:, None, :]
        decay = jnp.where(mask[None], jnp.exp(jnp.where(mask[None], diff, 0.0)), 0.0)
        weights = (
            scores[None] * decay * step_late[:, part_start : part_start + group].T[:, None, :]
        ).astype(jnp.bfloat16)
        pieces.append(
            jnp.einsum(
                "hts,shp->thp",
                weights,
                xs[:, part_start : part_start + group, :],
                preferred_element_type=jnp.float32,
            )
        )
    inner = jnp.concatenate(pieces, axis=1)
    carried = carry.astype(jnp.bfloat16)
    outer = (
        jnp.exp(cum)[:, :, None]
        * alive[:, None, None]
        * jnp.einsum("hpn,tn->thp", carried, cs, preferred_element_type=jnp.float32)
    )
    total_out = inner + outer + skip[None, :, None] * xs.astype(jnp.float32)
    normed = (
        total_out
        * lax.rsqrt(jnp.mean(total_out * total_out, axis=-1, keepdims=True) + 1e-05)
        * norm_gain.reshape(heads, head_dim)[None]
    )
    return normed.astype(jnp.bfloat16).reshape(rows, inner_width)


def solution(mesh):
    in_specs = (
        P(("dp", "ctx"), None),
        P(("dp", "ctx"), None),
        P("dp"),
        P(),
        P(),
        P(),
        P(),
        P(),
        P(),
    )
    out_specs = P(("dp", "ctx"), None)
    return jax.shard_map(body, mesh=mesh, in_specs=in_specs, out_specs=out_specs, check_vma=False)
```

```python
import jax
import jax.numpy as jnp
from jax import lax
from jax.sharding import PartitionSpec as P


def shifted(block, axis, distance):
    devices = range(lax.axis_size(axis))
    route = [(i - distance, i) for i in devices if i - distance in devices]
    return lax.ppermute(block, axis, route)


def packed(decay, local):
    lanes = local.shape[-1]
    flat = local.reshape(-1, lanes)
    spare = jnp.pad(decay, (0, 8 * lanes - decay.shape[0])).reshape(8, lanes)
    return jnp.concatenate([flat, spare], axis=0)


def unpacked(block, heads, rest):
    rows = block.shape[0] - 8
    return (block[rows, :heads], block[:rows].reshape((heads,) + rest))


def chain_carry(decay, scaled, bs, held):
    size, position = (lax.axis_size("ctx"), lax.axis_index("ctx"))
    chips = size // 2
    core = position % 2
    low = core == 0
    heads = decay.shape[0]
    half = heads // 2
    rows = scaled.shape[0]
    width = half * scaled.shape[2]
    swap = [(2 * i + j, 2 * i + 1 - j) for i in range(chips) for j in range(2)]
    front, back = scaled[:, :half], scaled[:, half:]
    mine_x = jnp.where(low, front, back)
    theirs_x = jnp.where(low, back, front)
    mine = jnp.einsum("shp,sn->hpn", mine_x, bs, preferred_element_type=jnp.float32)
    rest = mine.shape[1:]
    top = lax.reduce_precision(decay, exponent_bits=8, mantissa_bits=7)
    middle = lax.reduce_precision(decay - top, exponent_bits=8, mantissa_bits=7)
    bottom = lax.reduce_precision(decay - top - middle, exponent_bits=8, mantissa_bits=7)
    split = jnp.stack([top, middle, bottom]).astype(jnp.bfloat16)
    pieces = jnp.zeros((rows, bs.shape[1]), jnp.bfloat16).at[:3, :heads].set(split)
    got = lax.ppermute(
        jnp.concatenate([theirs_x.reshape(rows, width), bs, pieces], axis=1), "ctx", swap
    )
    got_x = got[:, :width].reshape(scaled.shape[0], half, scaled.shape[2])
    got_b = got[:, width : width + bs.shape[1]]
    spare = got[:3, width + bs.shape[1] : width + bs.shape[1] + heads].astype(jnp.float32)
    got_decay = (spare[0] + spare[1]) + spare[2]
    got_local = jnp.einsum("shp,sn->hpn", got_x, got_b, preferred_element_type=jnp.float32)
    decay_hi = lax.dynamic_slice_in_dim(jnp.where(low, got_decay, decay), core * half, half, 0)
    decay_lo = lax.dynamic_slice_in_dim(jnp.where(low, decay, got_decay), core * half, half, 0)
    local_lo = jnp.where(low, mine, got_local)
    local_hi = jnp.where(low, got_local, mine)
    chip_decay = decay_hi * decay_lo
    chip_local = decay_hi[:, None, None] * local_lo + local_hi
    one = [(i, i + 2) for i in range(size - 2)]
    two = [(i, i + 4) for i in range(size - 4)]
    sent, held = lax.optimization_barrier((packed(chip_decay, chip_local), held))
    first_hop = lax.ppermute(sent, "ctx", one)
    decay_a, local_a = unpacked(first_hop, half, rest)
    decay_b, local_b = unpacked(lax.ppermute(first_hop.astype(jnp.bfloat16), "ctx", one).astype(jnp.float32), half, rest)
    decay_ab = decay_a * decay_b
    local_ab = decay_a[:, None, None] * local_b + local_a
    local_c = lax.ppermute(local_ab.astype(jnp.bfloat16), "ctx", two).astype(jnp.float32)
    carry_half = decay_ab[:, None, None] * local_c + local_ab
    onward = decay_lo[:, None, None] * carry_half + local_lo
    got_end = lax.ppermute(jnp.where(low, onward, carry_half), "ctx", swap)
    first = jnp.where(low, carry_half, got_end)
    second = jnp.where(low, got_end, onward)
    return (jnp.concatenate([first, second], axis=0), held)


def body(xbc, dt_raw, lengths, conv_weight, conv_bias, dt_bias, decay_rate, skip, norm_gain):
    rows = xbc.shape[0]
    heads = dt_raw.shape[1]
    inner_width = norm_gain.shape[0]
    head_dim = inner_width // heads
    state_dim = (xbc.shape[1] - inner_width) // 2
    taps = conv_weight.shape[0]
    device = lax.axis_index("ctx")
    first = device * rows
    docs = lengths.shape[0]
    order = jnp.arange(docs, dtype=jnp.int32)
    ends = jnp.sum(jnp.where(order[None, :] <= order[:, None], lengths[None, :], 0), axis=1)
    halo = 16
    places = first - halo + jnp.arange(rows + halo, dtype=jnp.int32)
    counted = jnp.sum((places[:, None] >= ends[None, :]).astype(jnp.int32), axis=1)
    seg_wide = jnp.where(places < 0, -1, counted)
    seg = seg_wide[halo:]
    rim = shifted(xbc[rows - halo :], "ctx", 1)
    widened = jnp.concatenate([rim, xbc], axis=0)
    total = conv_bias[None, :] + conv_weight[taps - 1][None, :] * xbc.astype(jnp.float32)
    for lag in range(1, taps):
        moved = widened[halo - lag : halo - lag + rows].astype(jnp.float32)
        same = seg_wide[halo - lag : halo - lag + rows] == seg
        total = total + conv_weight[taps - 1 - lag][None, :] * jnp.where(same[:, None], moved, 0.0)
    act = jax.nn.silu(total).astype(jnp.bfloat16)
    xs = act[:, :inner_width].reshape(rows, heads, head_dim)
    bs = act[:, inner_width : inner_width + state_dim]
    cs = act[:, inner_width + state_dim :]
    step_size = jax.nn.softplus(dt_raw + dt_bias[None, :])
    cum = jnp.cumsum(-step_size * decay_rate[None, :], axis=0)
    alive = (seg == seg_wide[halo - 1]).astype(jnp.float32)
    same_end = (seg == seg[-1]).astype(jnp.float32)
    factor = jnp.exp(cum[-1][None, :] - cum) * same_end[:, None] * step_size
    scaled = (factor[:, :, None] * xs.astype(jnp.float32)).astype(jnp.bfloat16)
    block_decay = jnp.exp(cum[-1]) * alive[-1]
    carry, (cum_late, step_late, seg_late) = chain_carry(block_decay, scaled, bs, (cum, step_size, seg))
    scores = jnp.dot(cs, bs.T, preferred_element_type=jnp.float32)
    index = jnp.arange(rows, dtype=jnp.int32)
    mask = (index[:, None] >= index[None, :]) & (seg_late[:, None] == seg_late[None, :])
    group = 8
    pieces = []
    for part_start in range(0, heads, group):
        cum_part = cum_late[:, part_start : part_start + group].T
        diff = cum_part[:, :, None] - cum_part[:, None, :]
        decay = jnp.where(mask[None], jnp.exp(jnp.where(mask[None], diff, 0.0)), 0.0)
        weights = (
            scores[None] * decay * step_late[:, part_start : part_start + group].T[:, None, :]
        ).astype(jnp.bfloat16)
        pieces.append(
            jnp.einsum(
                "hts,shp->thp",
                weights,
                xs[:, part_start : part_start + group, :],
                preferred_element_type=jnp.float32,
            )
        )
    inner = jnp.concatenate(pieces, axis=1)
    carried = carry.astype(jnp.bfloat16)
    outer = (
        jnp.exp(cum)[:, :, None]
        * alive[:, None, None]
        * jnp.einsum("hpn,tn->thp", carried, cs, preferred_element_type=jnp.float32)
    )
    total_out = inner + outer + skip[None, :, None] * xs.astype(jnp.float32)
    normed = (
        total_out
        * lax.rsqrt(jnp.mean(total_out * total_out, axis=-1, keepdims=True) + 1e-05)
        * norm_gain.reshape(heads, head_dim)[None]
    )
    return normed.astype(jnp.bfloat16).reshape(rows, inner_width)


def solution(mesh):
    in_specs = (
        P(("dp", "ctx"), None),
        P(("dp", "ctx"), None),
        P("dp"),
        P(),
        P(),
        P(),
        P(),
        P(),
        P(),
    )
    out_specs = P(("dp", "ctx"), None)
    return jax.shard_map(body, mesh=mesh, in_specs=in_specs, out_specs=out_specs, check_vma=False)
```

```python
import jax
import jax.numpy as jnp
from jax import lax
from jax.sharding import PartitionSpec as P


def shifted(block, axis, distance):
    devices = range(lax.axis_size(axis))
    route = [(i - distance, i) for i in devices if i - distance in devices]
    return lax.ppermute(block, axis, route)


def packed(decay, local):
    lanes = local.shape[-1]
    flat = local.reshape(-1, lanes)
    spare = jnp.pad(decay, (0, 8 * lanes - decay.shape[0])).reshape(8, lanes)
    return jnp.concatenate([flat, spare], axis=0)


def unpacked(block, heads, rest):
    rows = block.shape[0] - 8
    return (block[rows, :heads], block[:rows].reshape((heads,) + rest))


def chain_carry(decay, scaled, bs, held):
    size, position = (lax.axis_size("ctx"), lax.axis_index("ctx"))
    chips = size // 2
    core = position % 2
    low = core == 0
    heads = decay.shape[0]
    half = heads // 2
    rows = scaled.shape[0]
    width = half * scaled.shape[2]
    swap = [(2 * i + j, 2 * i + 1 - j) for i in range(chips) for j in range(2)]
    front, back = scaled[:, :half], scaled[:, half:]
    mine_x = jnp.where(low, front, back)
    theirs_x = jnp.where(low, back, front)
    mine = jnp.einsum("shp,sn->hpn", mine_x, bs, preferred_element_type=jnp.float32)
    rest = mine.shape[1:]
    top = lax.reduce_precision(decay, exponent_bits=8, mantissa_bits=7)
    middle = lax.reduce_precision(decay - top, exponent_bits=8, mantissa_bits=7)
    bottom = lax.reduce_precision(decay - top - middle, exponent_bits=8, mantissa_bits=7)
    split = jnp.stack([top, middle, bottom]).astype(jnp.bfloat16)
    pieces = jnp.zeros((rows, bs.shape[1]), jnp.bfloat16).at[:3, :heads].set(split)
    got = lax.ppermute(
        jnp.concatenate([theirs_x.reshape(rows, width), bs, pieces], axis=1), "ctx", swap
    )
    got_x = got[:, :width]
    got_b = got[:, width : width + bs.shape[1]]
    spare = got[:3, width + bs.shape[1] : width + bs.shape[1] + heads].astype(jnp.float32)
    got_decay = (spare[0] + spare[1]) + spare[2]
    got_local = jnp.einsum("sk,sn->kn", got_x, got_b, preferred_element_type=jnp.float32).reshape(
        (half,) + rest
    )
    decay_hi = lax.dynamic_slice_in_dim(jnp.where(low, got_decay, decay), core * half, half, 0)
    decay_lo = lax.dynamic_slice_in_dim(jnp.where(low, decay, got_decay), core * half, half, 0)
    local_lo = jnp.where(low, mine, got_local)
    local_hi = jnp.where(low, got_local, mine)
    chip_decay = decay_hi * decay_lo
    chip_local = decay_hi[:, None, None] * local_lo + local_hi
    one = [(i, i + 2) for i in range(size - 2)]
    two = [(i, i + 4) for i in range(size - 4)]
    sent, held = lax.optimization_barrier((packed(chip_decay, chip_local), held))
    first_hop = lax.ppermute(sent, "ctx", one)
    decay_a, local_a = unpacked(first_hop, half, rest)
    decay_b, local_b = unpacked(lax.ppermute(first_hop.astype(jnp.bfloat16), "ctx", one).astype(jnp.float32), half, rest)
    decay_ab = decay_a * decay_b
    local_ab = decay_a[:, None, None] * local_b + local_a
    local_c = lax.ppermute(local_ab.astype(jnp.bfloat16), "ctx", two).astype(jnp.float32)
    carry_half = decay_ab[:, None, None] * local_c + local_ab
    onward = decay_lo[:, None, None] * carry_half + local_lo
    got_end = lax.ppermute(jnp.where(low, onward, carry_half), "ctx", swap)
    first = jnp.where(low, carry_half, got_end)
    second = jnp.where(low, got_end, onward)
    return (jnp.concatenate([first, second], axis=0), held)


def body(xbc, dt_raw, lengths, conv_weight, conv_bias, dt_bias, decay_rate, skip, norm_gain):
    rows = xbc.shape[0]
    heads = dt_raw.shape[1]
    inner_width = norm_gain.shape[0]
    head_dim = inner_width // heads
    state_dim = (xbc.shape[1] - inner_width) // 2
    taps = conv_weight.shape[0]
    device = lax.axis_index("ctx")
    first = device * rows
    docs = lengths.shape[0]
    order = jnp.arange(docs, dtype=jnp.int32)
    ends = jnp.sum(jnp.where(order[None, :] <= order[:, None], lengths[None, :], 0), axis=1)
    halo = 16
    places = first - halo + jnp.arange(rows + halo, dtype=jnp.int32)
    counted = jnp.sum((places[:, None] >= ends[None, :]).astype(jnp.int32), axis=1)
    seg_wide = jnp.where(places < 0, -1, counted)
    seg = seg_wide[halo:]
    rim = shifted(xbc[rows - halo :], "ctx", 1)
    widened = jnp.concatenate([rim, xbc], axis=0)
    total = conv_bias[None, :] + conv_weight[taps - 1][None, :] * xbc.astype(jnp.float32)
    for lag in range(1, taps):
        moved = widened[halo - lag : halo - lag + rows].astype(jnp.float32)
        same = seg_wide[halo - lag : halo - lag + rows] == seg
        total = total + conv_weight[taps - 1 - lag][None, :] * jnp.where(same[:, None], moved, 0.0)
    act = jax.nn.silu(total).astype(jnp.bfloat16)
    xs = act[:, :inner_width].reshape(rows, heads, head_dim)
    bs = act[:, inner_width : inner_width + state_dim]
    cs = act[:, inner_width + state_dim :]
    step_size = jax.nn.softplus(dt_raw + dt_bias[None, :])
    cum = jnp.cumsum(-step_size * decay_rate[None, :], axis=0)
    alive = (seg == seg_wide[halo - 1]).astype(jnp.float32)
    same_end = (seg == seg[-1]).astype(jnp.float32)
    factor = jnp.exp(cum[-1][None, :] - cum) * same_end[:, None] * step_size
    scaled = (factor[:, :, None] * xs.astype(jnp.float32)).astype(jnp.bfloat16)
    block_decay = jnp.exp(cum[-1]) * alive[-1]
    carry, (cum_late, step_late, seg_late) = chain_carry(block_decay, scaled, bs, (cum, step_size, seg))
    scores = jnp.dot(cs, bs.T, preferred_element_type=jnp.float32)
    index = jnp.arange(rows, dtype=jnp.int32)
    mask = (index[:, None] >= index[None, :]) & (seg_late[:, None] == seg_late[None, :])
    group = 8
    pieces = []
    for part_start in range(0, heads, group):
        cum_part = cum_late[:, part_start : part_start + group].T
        diff = cum_part[:, :, None] - cum_part[:, None, :]
        decay = jnp.where(mask[None], jnp.exp(jnp.where(mask[None], diff, 0.0)), 0.0)
        weights = (
            scores[None] * decay * step_late[:, part_start : part_start + group].T[:, None, :]
        ).astype(jnp.bfloat16)
        pieces.append(
            jnp.einsum(
                "hts,shp->thp",
                weights,
                xs[:, part_start : part_start + group, :],
                preferred_element_type=jnp.float32,
            )
        )
    inner = jnp.concatenate(pieces, axis=1)
    carried = carry.astype(jnp.bfloat16)
    outer = (
        jnp.exp(cum)[:, :, None]
        * alive[:, None, None]
        * jnp.einsum("hpn,tn->thp", carried, cs, preferred_element_type=jnp.float32)
    )
    total_out = inner + outer + skip[None, :, None] * xs.astype(jnp.float32)
    normed = (
        total_out
        * lax.rsqrt(jnp.mean(total_out * total_out, axis=-1, keepdims=True) + 1e-05)
        * norm_gain.reshape(heads, head_dim)[None]
    )
    return normed.astype(jnp.bfloat16).reshape(rows, inner_width)


def solution(mesh):
    in_specs = (
        P(("dp", "ctx"), None),
        P(("dp", "ctx"), None),
        P("dp"),
        P(),
        P(),
        P(),
        P(),
        P(),
        P(),
    )
    out_specs = P(("dp", "ctx"), None)
    return jax.shard_map(body, mesh=mesh, in_specs=in_specs, out_specs=out_specs, check_vma=False)
```

```python
import jax
import jax.numpy as jnp
from jax import lax
from jax.sharding import PartitionSpec as P


def shifted(block, axis, distance):
    devices = range(lax.axis_size(axis))
    route = [(i - distance, i) for i in devices if i - distance in devices]
    return lax.ppermute(block, axis, route)


def packed(decay, local):
    lanes = local.shape[-1]
    flat = local.reshape(-1, lanes)
    spare = jnp.pad(decay, (0, 8 * lanes - decay.shape[0])).reshape(8, lanes)
    return jnp.concatenate([flat, spare], axis=0)


def unpacked(block, heads, rest):
    rows = block.shape[0] - 8
    return (block[rows, :heads], block[:rows].reshape((heads,) + rest))


def chain_carry(decay, scaled, bs, held):
    size, position = (lax.axis_size("ctx"), lax.axis_index("ctx"))
    chips = size // 2
    core = position % 2
    low = core == 0
    heads = decay.shape[0]
    half = heads // 2
    rows = scaled.shape[0]
    width = half * scaled.shape[2]
    swap = [(2 * i + j, 2 * i + 1 - j) for i in range(chips) for j in range(2)]
    flat = scaled.reshape(rows, 2 * width)
    front, back = flat[:, :width], flat[:, width:]
    mine_x = jnp.where(low, front, back)
    theirs_x = jnp.where(low, back, front)
    rest = scaled.shape[2:] + bs.shape[1:]
    mine = jnp.einsum("sk,sn->kn", mine_x, bs, preferred_element_type=jnp.float32).reshape((half,) + rest)
    top = lax.reduce_precision(decay, exponent_bits=8, mantissa_bits=7)
    middle = lax.reduce_precision(decay - top, exponent_bits=8, mantissa_bits=7)
    bottom = lax.reduce_precision(decay - top - middle, exponent_bits=8, mantissa_bits=7)
    split = jnp.stack([top, middle, bottom]).astype(jnp.bfloat16)
    pieces = jnp.zeros((rows, bs.shape[1]), jnp.bfloat16).at[:3, :heads].set(split)
    got = lax.ppermute(
        jnp.concatenate([theirs_x, bs, pieces], axis=1), "ctx", swap
    )
    got_x = got[:, :width]
    got_b = got[:, width : width + bs.shape[1]]
    spare = got[:3, width + bs.shape[1] : width + bs.shape[1] + heads].astype(jnp.float32)
    got_decay = (spare[0] + spare[1]) + spare[2]
    got_local = jnp.einsum("sk,sn->kn", got_x, got_b, preferred_element_type=jnp.float32).reshape(
        (half,) + rest
    )
    decay_hi = lax.dynamic_slice_in_dim(jnp.where(low, got_decay, decay), core * half, half, 0)
    decay_lo = lax.dynamic_slice_in_dim(jnp.where(low, decay, got_decay), core * half, half, 0)
    local_lo = jnp.where(low, mine, got_local)
    local_hi = jnp.where(low, got_local, mine)
    chip_decay = decay_hi * decay_lo
    chip_local = decay_hi[:, None, None] * local_lo + local_hi
    one = [(i, i + 2) for i in range(size - 2)]
    two = [(i, i + 4) for i in range(size - 4)]
    sent, held = lax.optimization_barrier((packed(chip_decay, chip_local), held))
    first_hop = lax.ppermute(sent, "ctx", one)
    decay_a, local_a = unpacked(first_hop, half, rest)
    decay_b, local_b = unpacked(lax.ppermute(first_hop.astype(jnp.bfloat16), "ctx", one).astype(jnp.float32), half, rest)
    decay_ab = decay_a * decay_b
    local_ab = decay_a[:, None, None] * local_b + local_a
    local_c = lax.ppermute(local_ab.astype(jnp.bfloat16), "ctx", two).astype(jnp.float32)
    carry_half = decay_ab[:, None, None] * local_c + local_ab
    onward = decay_lo[:, None, None] * carry_half + local_lo
    got_end = lax.ppermute(jnp.where(low, onward, carry_half), "ctx", swap)
    first = jnp.where(low, carry_half, got_end)
    second = jnp.where(low, got_end, onward)
    return (jnp.concatenate([first, second], axis=0), held)


def body(xbc, dt_raw, lengths, conv_weight, conv_bias, dt_bias, decay_rate, skip, norm_gain):
    rows = xbc.shape[0]
    heads = dt_raw.shape[1]
    inner_width = norm_gain.shape[0]
    head_dim = inner_width // heads
    state_dim = (xbc.shape[1] - inner_width) // 2
    taps = conv_weight.shape[0]
    device = lax.axis_index("ctx")
    first = device * rows
    docs = lengths.shape[0]
    order = jnp.arange(docs, dtype=jnp.int32)
    ends = jnp.sum(jnp.where(order[None, :] <= order[:, None], lengths[None, :], 0), axis=1)
    halo = 16
    places = first - halo + jnp.arange(rows + halo, dtype=jnp.int32)
    counted = jnp.sum((places[:, None] >= ends[None, :]).astype(jnp.int32), axis=1)
    seg_wide = jnp.where(places < 0, -1, counted)
    seg = seg_wide[halo:]
    rim = shifted(xbc[rows - halo :], "ctx", 1)
    widened = jnp.concatenate([rim, xbc], axis=0)
    total = conv_bias[None, :] + conv_weight[taps - 1][None, :] * xbc.astype(jnp.float32)
    for lag in range(1, taps):
        moved = widened[halo - lag : halo - lag + rows].astype(jnp.float32)
        same = seg_wide[halo - lag : halo - lag + rows] == seg
        total = total + conv_weight[taps - 1 - lag][None, :] * jnp.where(same[:, None], moved, 0.0)
    act = jax.nn.silu(total).astype(jnp.bfloat16)
    xs = act[:, :inner_width].reshape(rows, heads, head_dim)
    bs = act[:, inner_width : inner_width + state_dim]
    cs = act[:, inner_width + state_dim :]
    step_size = jax.nn.softplus(dt_raw + dt_bias[None, :])
    cum = jnp.cumsum(-step_size * decay_rate[None, :], axis=0)
    alive = (seg == seg_wide[halo - 1]).astype(jnp.float32)
    same_end = (seg == seg[-1]).astype(jnp.float32)
    factor = jnp.exp(cum[-1][None, :] - cum) * same_end[:, None] * step_size
    scaled = (factor[:, :, None] * xs.astype(jnp.float32)).astype(jnp.bfloat16)
    block_decay = jnp.exp(cum[-1]) * alive[-1]
    carry, (cum_late, step_late, seg_late) = chain_carry(block_decay, scaled, bs, (cum, step_size, seg))
    scores = jnp.dot(cs, bs.T, preferred_element_type=jnp.float32)
    index = jnp.arange(rows, dtype=jnp.int32)
    mask = (index[:, None] >= index[None, :]) & (seg_late[:, None] == seg_late[None, :])
    group = 8
    pieces = []
    for part_start in range(0, heads, group):
        cum_part = cum_late[:, part_start : part_start + group].T
        diff = cum_part[:, :, None] - cum_part[:, None, :]
        decay = jnp.where(mask[None], jnp.exp(jnp.where(mask[None], diff, 0.0)), 0.0)
        weights = (
            scores[None] * decay * step_late[:, part_start : part_start + group].T[:, None, :]
        ).astype(jnp.bfloat16)
        pieces.append(
            jnp.einsum(
                "hts,shp->thp",
                weights,
                xs[:, part_start : part_start + group, :],
                preferred_element_type=jnp.float32,
            )
        )
    inner = jnp.concatenate(pieces, axis=1)
    carried = carry.astype(jnp.bfloat16)
    outer = (
        jnp.exp(cum)[:, :, None]
        * alive[:, None, None]
        * jnp.einsum("hpn,tn->thp", carried, cs, preferred_element_type=jnp.float32)
    )
    total_out = inner + outer + skip[None, :, None] * xs.astype(jnp.float32)
    normed = (
        total_out
        * lax.rsqrt(jnp.mean(total_out * total_out, axis=-1, keepdims=True) + 1e-05)
        * norm_gain.reshape(heads, head_dim)[None]
    )
    return normed.astype(jnp.bfloat16).reshape(rows, inner_width)


def solution(mesh):
    in_specs = (
        P(("dp", "ctx"), None),
        P(("dp", "ctx"), None),
        P("dp"),
        P(),
        P(),
        P(),
        P(),
        P(),
        P(),
    )
    out_specs = P(("dp", "ctx"), None)
    return jax.shard_map(body, mesh=mesh, in_specs=in_specs, out_specs=out_specs, check_vma=False)
```
